32 devices in a mesh: scene: 2 (over y), step: 4 (over x, core), seq: 4 (over z).
Axes of the slice: x: 2, y: 2, z: 4, core: 2. Of those that a mesh axis runs over, the one named last changes fastest.
Arguments:
- queries: bfloat16 [32, 2, 24, 32, 128], P(('scene', 'step'), None, None, 'seq'), parts along dimension 0, may hold values from -256 to 256
- keys: bfloat16 [32, 2, 24, 32, 128], P(('scene', 'step'), None, None, 'seq'), parts along dimension 0, may hold values from -8 to 8
- values: bfloat16 [32, 2, 24, 32, 128], P(('scene', 'step'), None, None, 'seq'), parts along dimension 0, may hold values from -6 to 6
- start_latent: float32 [128, 32], P('scene', 'seq'), parts along dimension 0, may hold values from -6 to 6
- out_weight: bfloat16 [64, 3072], replicated, may hold values from -0.109375 to 0.109375
- cfg_table: float32 [8], replicated, may hold values from 3 to 8
- cfg_index: int32 [2], P('scene'), parts along dimension 0, may hold values from 0 to 7
- step_table: float32 [1000], replicated, may hold values from 0.03 to 0.12
- time_index: int32 [32], P(('scene', 'step')), parts along dimension 0, may hold values from 0 to 999
Outputs:
- new_iterates: float32 [32, 64, 32], P(('scene', 'step'), None, 'seq'), parts along dimension 0
The draws below stay inside these ranges and needn't reach their ends.
There are 2 independent parts, one for each index of `scene`. The reference program is written for one: setup_inputs(seed, part) draws one part's arguments, and reference() takes and returns one part's arrays. A program takes and returns all parts, laid end to end along the dimension named above; an argument that names none is the same for every part. Nothing has to cross between parts.
All inputs are finite; a program needn't handle non-finite values.
Results may differ from the reference program's by a relative error of at most 0.0034.
Values may be sent and summed in bfloat16 or wider, within the bound.
No kernel may reach another device: no remote copies, remote signals or barrier semaphores. Data moves between devices by JAX's collectives and lax.ppermute only.
A program may use at most 64 MiB of HBM per device.

```python
import math
import jax
import jax.numpy as jnp
from jax import lax

HD = 128
C = 64
H = 24
G = 8
NT = 1000
STEPS = 16
LEN = 32


def pair_draw(key):
    query_key = jax.random.fold_in(key, 101)
    key_key = jax.random.fold_in(key, 202)
    shape = (STEPS, 2, H, LEN, HD)
    query_all = jax.random.normal(query_key, shape, jnp.float32)
    key_all = jax.random.normal(key_key, shape, jnp.float32)
    return (query_all, key_all)


def draw_queries(key, part):
    return pair_draw(key)[0].astype(jnp.bfloat16)


def draw_keys(key, part):
    return pair_draw(key)[1].astype(jnp.bfloat16)


def place_ends(array, key, smallest, top_value):
    spot = [jax.random.randint(jax.random.fold_in(key, axis), (), 0, length) for axis, length in enumerate(array.shape)]
    widest = array.shape.index(max(array.shape))
    beside = spot[:widest] + [(spot[widest] + 1) % array.shape[widest]] + spot[widest + 1:]
    return array.at[tuple(spot)].set(smallest).at[tuple(beside)].set(top_value)


def levels(key, extent, split, low, high):
    def one(position, parts):
        steps = jax.random.uniform(jax.random.fold_in(jax.random.fold_in(key, 6), position), (parts,), jnp.float32, low / len(split), high / len(split))
        return jnp.repeat(jnp.exp(steps), extent[position] // parts).reshape((-1,) + (1,) * (len(extent) - position - 1))

    factor_of = one(*split[0])
    for cut in split[1:]:
        factor_of = factor_of * one(*cut)
    return factor_of


def gaussian(rng, extent, width, most, split=(), kind=jnp.bfloat16):
    entries = width * jax.random.normal(rng, extent, jnp.float32)
    if split:
        entries = entries * levels(rng, extent, split, -0.22, 0.18)
    return jnp.clip(entries, -most, most).astype(kind)


def setup_inputs(seed: int = 0, part: int = 0) -> dict:
    key_list = jax.random.split(jax.random.key(seed), 10)
    part_splits = jax.random.split(jax.random.fold_in(key_list[9], part), 10)
    queries = draw_queries(jax.random.fold_in(jax.random.fold_in(key_list[9], part), 71), part)
    keys = draw_keys(jax.random.fold_in(jax.random.fold_in(key_list[9], part), 71), part)
    values = gaussian(part_splits[2], (STEPS, 2, H, LEN, HD), 1.0, 6.0, ((0, 4), (3, 4)))
    start_latent = gaussian(part_splits[3], (C, LEN), 1.0, 6.0, ((1, 4),), jnp.float32)
    out_weight = gaussian(key_list[4], (C, H * HD), (H * HD) ** -0.5, 0.109375)
    cfg_table = jnp.clip(jax.random.uniform(key_list[5], (G,), jnp.float32, 3.0, 8.0), 3.0, 8.0)
    cfg_index = jax.random.randint(part_splits[6], (1,), 0, G).astype(jnp.int32)
    step_table = jnp.clip(jnp.exp(jax.random.uniform(key_list[7], (NT,), jnp.float32, math.log(0.03), math.log(0.12))), 0.03, 0.12)
    time_index = place_ends(jax.random.randint(part_splits[8], (STEPS,), 0, NT), jax.random.fold_in(part_splits[8], 1), 0, NT - 1).astype(jnp.int32)
    return dict(queries=queries, keys=keys, values=values, start_latent=start_latent, out_weight=out_weight, cfg_table=cfg_table, cfg_index=cfg_index, step_table=step_table, time_index=time_index)


def lookup(table, index):
    count = table.shape[0]
    hits = index[..., None] == jnp.arange(count, dtype=jnp.int32)
    return lax.optimization_barrier(jnp.sum(jnp.where(hits, table, jnp.zeros((), table.dtype)), axis=-1))

def attend(query_rows, key_rows, value_rows):
    length = query_rows.shape[0]
    block_rows = min(512, length)
    scale = HD ** (-0.5)

    def one_block(query_block):
        scores = jnp.dot(query_block, key_rows.T, preferred_element_type=jnp.float32) * scale
        expo = jnp.exp(scores - lax.optimization_barrier(jnp.max(scores, axis=-1, keepdims=True)))
        total = lax.optimization_barrier(jnp.sum(expo, axis=-1, keepdims=True))
        weights = expo.astype(jnp.bfloat16)
        return (jnp.dot(weights, value_rows, preferred_element_type=jnp.float32) / total).astype(jnp.bfloat16)
    blocks = query_rows.reshape(length // block_rows, block_rows, query_rows.shape[1])
    return lax.map(one_block, blocks).reshape(query_rows.shape)

def reference(queries, keys, values, start_latent, out_weight, cfg_table, cfg_index, step_table, time_index):
    flat_q = queries.reshape(-1, LEN, HD)
    flat_k = keys.reshape(-1, LEN, HD)
    flat_v = values.reshape(-1, LEN, HD)
    heads_out = lax.map(lambda trio: attend(trio[0], trio[1], trio[2]), (flat_q, flat_k, flat_v))
    heads_out = heads_out.reshape(STEPS, 2, H, LEN, HD).astype(jnp.float32)
    square_sum = lax.optimization_barrier(jnp.sum(heads_out * heads_out, axis=(2, 4)))
    root_mean = jnp.sqrt(square_sum / (H * HD) + 1e-06)
    weight_heads = out_weight.reshape(C, H, HD).astype(jnp.float32)
    drift = jnp.einsum('chd,sbhld->sbcl', weight_heads, heads_out) / root_mean[:, :, None, :]
    scale = lookup(cfg_table, cfg_index)[0]
    guided = drift[:, 1] + scale * (drift[:, 0] - drift[:, 1])
    step_len = lookup(step_table, time_index)
    return start_latent[None] + jnp.cumsum(step_len[:, None, None] * guided, axis=0)
```

```python
import jax
import jax.numpy as jnp
from jax import lax
from jax.sharding import PartitionSpec as P

HD = 128
H = 24


def lookup(table, index):
    count = table.shape[0]
    hits = index[..., None] == jnp.arange(count, dtype=jnp.int32)
    return jnp.sum(jnp.where(hits, table, jnp.zeros((), table.dtype)), axis=-1)


def attend(query_rows, key_rows, value_rows):
    scale = HD ** (-0.5)
    scores = (
        jnp.einsum("iqd,ikd->iqk", query_rows, key_rows, preferred_element_type=jnp.float32) * scale
    )
    expo = jnp.exp(scores - jnp.max(scores, axis=-1, keepdims=True))
    total = jnp.sum(expo, axis=-1, keepdims=True)
    weights = expo.astype(jnp.bfloat16)
    out = jnp.einsum("iqk,ikd->iqd", weights, value_rows, preferred_element_type=jnp.float32)
    return (out / total).astype(jnp.bfloat16)


def on_device(
    queries, keys, values, start_latent, out_weight, cfg_table, cfg_index, step_table, time_index
):
    step_dev, branches, heads, tok_dev, head_size = queries.shape
    groups = lax.axis_size("seq")
    steps_axis = lax.axis_size("step")
    items = step_dev * branches * heads
    per_dev = items // groups
    length = tok_dev * groups
    channels = out_weight.shape[0]
    me = lax.axis_index("seq")

    stacked = jnp.stack([queries, keys, values]).reshape(3, groups, per_dev, tok_dev, head_size)
    gathered = lax.all_to_all(stacked, "seq", split_axis=1, concat_axis=3, tiled=True)
    gathered = gathered.reshape(3, per_dev, length, head_size)
    heads_out = attend(gathered[0], gathered[1], gathered[2])

    weight_heads = out_weight.reshape(channels, heads, head_size)
    guide_scale = lookup(cfg_table, cfg_index)[0]
    step_len = lookup(step_table, time_index)

    if per_dev % (branches * heads) == 0:
        local_steps = per_dev // (branches * heads)
        ho = heads_out.reshape(local_steps, branches, heads, length, head_size)
        wide = ho.astype(jnp.float32)
        square_sum = jnp.sum(wide * wide, axis=(2, 4))
        root_mean = jnp.sqrt(square_sum / (H * HD) + 1e-06)
        drift = (
            jnp.einsum("chd,sbhld->sbcl", weight_heads, ho, preferred_element_type=jnp.float32)
            / root_mean[:, :, None, :]
        )
        guided = drift[:, 1] + guide_scale * (drift[:, 0] - drift[:, 1])
        my_len = lax.dynamic_slice_in_dim(step_len, me * local_steps, local_steps)
        update = my_len[:, None, None] * guided
        every = lax.all_gather(update, ("step", "seq"), axis=0, tiled=True)
        prefix = jnp.cumsum(every, axis=0)
        position = lax.axis_index("step")
        mine = lax.dynamic_slice_in_dim(prefix, position * step_dev, step_dev, axis=0)
        mine = lax.dynamic_slice_in_dim(mine, me * tok_dev, tok_dev, axis=2)
        return start_latent[None] + mine

    assert heads % per_dev == 0
    share = heads // per_dev
    first = me * per_dev
    head_ids = (first + jnp.arange(per_dev, dtype=jnp.int32)) % heads
    chosen = jnp.take(weight_heads, head_ids, axis=1)
    numer = jnp.einsum("cid,ild->cl", chosen, heads_out, preferred_element_type=jnp.float32)
    wide = heads_out.astype(jnp.float32)
    square = jnp.sum(wide * wide, axis=(0, 2))
    partial = jnp.concatenate([numer, square[None]], axis=0)
    partial = partial.reshape(channels + 1, groups, tok_dev)
    returned = lax.all_to_all(partial, "seq", split_axis=1, concat_axis=1, tiled=True)
    returned = returned.reshape(channels + 1, step_dev * branches, share, tok_dev)
    summed = jnp.sum(returned, axis=2).reshape(channels + 1, step_dev, branches, tok_dev)
    numer = jnp.transpose(summed[:channels], (1, 2, 0, 3))
    square_sum = summed[channels]
    root_mean = jnp.sqrt(square_sum / (H * HD) + 1e-06)
    drift = numer / root_mean[:, :, None, :]
    guided = drift[:, 1] + guide_scale * (drift[:, 0] - drift[:, 1])
    local_cum = jnp.cumsum(step_len[:, None, None] * guided, axis=0)
    group_total = local_cum[-1]
    every_total = lax.all_gather(group_total[None], "step", axis=0, tiled=True)
    position = lax.axis_index("step")
    order = jnp.arange(steps_axis, dtype=jnp.int32)
    earlier = jnp.sum(
        jnp.where((order < position)[:, None, None], every_total, jnp.zeros((), jnp.float32)),
        axis=0,
    )
    return start_latent[None] + earlier[None] + local_cum


def solution(mesh):
    return jax.shard_map(
        on_device,
        mesh=mesh,
        in_specs=(
            P(("scene", "step"), None, None, "seq", None),
            P(("scene", "step"), None, None, "seq", None),
            P(("scene", "step"), None, None, "seq", None),
            P("scene", "seq"),
            P(),
            P(),
            P("scene"),
            P(),
            P(("scene", "step")),
        ),
        out_specs=P(("scene", "step"), None, "seq"),
        check_vma=False,
    )
```

```python
import jax
import jax.numpy as jnp
from jax import lax
from jax.sharding import PartitionSpec as P

HD = 128
H = 24


def lookup(table, index):
    count = table.shape[0]
    hits = index[..., None] == jnp.arange(count, dtype=jnp.int32)
    return jnp.sum(jnp.where(hits, table, jnp.zeros((), table.dtype)), axis=-1)


def attend(query_rows, key_rows, value_rows):
    scale = HD ** (-0.5)
    scores = (
        jnp.einsum("iqd,ikd->iqk", query_rows, key_rows, preferred_element_type=jnp.float32) * scale
    )
    expo = jnp.exp(scores - jnp.max(scores, axis=-1, keepdims=True))
    total = jnp.sum(expo, axis=-1, keepdims=True)
    weights = expo.astype(jnp.bfloat16)
    out = jnp.einsum("iqk,ikd->iqd", weights, value_rows, preferred_element_type=jnp.float32)
    return (out / total).astype(jnp.bfloat16)


def earlier_groups(local_cum, steps_axis):
    every_total = lax.all_gather(local_cum[-1][None], "step", axis=0, tiled=True)
    position = lax.axis_index("step")
    order = jnp.arange(steps_axis, dtype=jnp.int32)
    earlier = jnp.sum(
        jnp.where((order < position)[:, None, None], every_total, jnp.zeros((), jnp.float32)),
        axis=0,
    )
    return earlier[None]


def on_device(
    queries, keys, values, start_latent, out_weight, cfg_table, cfg_index, step_table, time_index
):
    step_dev, branches, heads, tok_dev, head_size = queries.shape
    groups = lax.axis_size("seq")
    steps_axis = lax.axis_size("step")
    items = step_dev * branches * heads
    per_dev = items // groups
    length = tok_dev * groups
    channels = out_weight.shape[0]
    me = lax.axis_index("seq")

    stacked = jnp.stack([queries, keys, values]).reshape(3, groups, per_dev, tok_dev, head_size)
    gathered = lax.all_to_all(stacked, "seq", split_axis=1, concat_axis=3, tiled=True)
    gathered = gathered.reshape(3, per_dev, length, head_size)
    heads_out = attend(gathered[0], gathered[1], gathered[2])

    weight_heads = out_weight.reshape(channels, heads, head_size)
    guide_scale = lookup(cfg_table, cfg_index)[0]
    step_len = lookup(step_table, time_index)

    if per_dev % (branches * heads) == 0:
        local_steps = per_dev // (branches * heads)
        ho = heads_out.reshape(local_steps, branches, heads, length, head_size)
        wide = ho.astype(jnp.float32)
        square_sum = jnp.sum(wide * wide, axis=(2, 4))
        root_mean = jnp.sqrt(square_sum / (H * HD) + 1e-06)
        drift = (
            jnp.einsum("chd,sbhld->sbcl", weight_heads, ho, preferred_element_type=jnp.float32)
            / root_mean[:, :, None, :]
        )
        guided = drift[:, 1] + guide_scale * (drift[:, 0] - drift[:, 1])
        my_len = lax.dynamic_slice_in_dim(step_len, me * local_steps, local_steps)
        update = my_len[:, None, None] * guided
        update = update.reshape(local_steps, channels, groups, tok_dev)
        local = lax.all_to_all(update, "seq", split_axis=2, concat_axis=0, tiled=True)
        local_cum = jnp.cumsum(local.reshape(step_dev, channels, tok_dev), axis=0)
        return start_latent[None] + earlier_groups(local_cum, steps_axis) + local_cum

    assert heads % per_dev == 0
    share = heads // per_dev
    first = me * per_dev
    head_ids = (first + jnp.arange(per_dev, dtype=jnp.int32)) % heads
    chosen = jnp.take(weight_heads, head_ids, axis=1)
    numer = jnp.einsum("cid,ild->cl", chosen, heads_out, preferred_element_type=jnp.float32)
    wide = heads_out.astype(jnp.float32)
    square = jnp.sum(wide * wide, axis=(0, 2))
    partial = jnp.concatenate([numer, square[None]], axis=0)
    partial = partial.reshape(channels + 1, groups, tok_dev)
    returned = lax.all_to_all(partial, "seq", split_axis=1, concat_axis=1, tiled=True)
    returned = returned.reshape(channels + 1, step_dev * branches, share, tok_dev)
    summed = jnp.sum(returned, axis=2).reshape(channels + 1, step_dev, branches, tok_dev)
    numer = jnp.transpose(summed[:channels], (1, 2, 0, 3))
    square_sum = summed[channels]
    root_mean = jnp.sqrt(square_sum / (H * HD) + 1e-06)
    drift = numer / root_mean[:, :, None, :]
    guided = drift[:, 1] + guide_scale * (drift[:, 0] - drift[:, 1])
    local_cum = jnp.cumsum(step_len[:, None, None] * guided, axis=0)
    return start_latent[None] + earlier_groups(local_cum, steps_axis) + local_cum


def solution(mesh):
    return jax.shard_map(
        on_device,
        mesh=mesh,
        in_specs=(
            P(("scene", "step"), None, None, "seq", None),
            P(("scene", "step"), None, None, "seq", None),
            P(("scene", "step"), None, None, "seq", None),
            P("scene", "seq"),
            P(),
            P(),
            P("scene"),
            P(),
            P(("scene", "step")),
        ),
        out_specs=P(("scene", "step"), None, "seq"),
        check_vma=False,
    )
```

```python
import jax
import jax.numpy as jnp
from jax import lax
from jax.sharding import PartitionSpec as P

HD = 128
H = 24


def lookup(table, index):
    count = table.shape[0]
    hits = index[..., None] == jnp.arange(count, dtype=jnp.int32)
    return jnp.sum(jnp.where(hits, table, jnp.zeros((), table.dtype)), axis=-1)


def attend(query_rows, key_rows, value_rows):
    scale = HD ** (-0.5)
    scores = (
        jnp.einsum("iqd,ikd->iqk", query_rows, key_rows, preferred_element_type=jnp.float32) * scale
    )
    expo = jnp.exp(scores - jnp.max(scores, axis=-1, keepdims=True))
    total = jnp.sum(expo, axis=-1, keepdims=True)
    weights = expo.astype(jnp.bfloat16)
    out = jnp.einsum("iqk,ikd->iqd", weights, value_rows, preferred_element_type=jnp.float32)
    return (out / total).astype(jnp.bfloat16)


def xor_pairs(size, k):
    return [(i, i ^ k) for i in range(size)]


def gather_prefix(update, me, groups, step_dev, steps_axis):
    local_steps = update.shape[0]
    partners = me ^ jnp.arange(groups, dtype=jnp.int32)
    ordered = jnp.take(update, partners, axis=2)
    pieces = [ordered[:, :, 0]]
    sources = [me]
    for k in range(1, groups):
        pieces.append(lax.ppermute(ordered[:, :, k], "seq", xor_pairs(groups, k)))
        sources.append(me ^ k)
    zero = jnp.zeros((), jnp.float32)
    outs = []
    for s in range(step_dev):
        acc = None
        for piece, source in zip(pieces, sources):
            for t in range(local_steps):
                term = jnp.where(source * local_steps + t <= s, piece[t], zero)
                acc = term if acc is None else acc + term
        outs.append(acc)
    local_cum = jnp.stack(outs)
    total = outs[-1]
    position = lax.axis_index("step")
    earlier = jnp.zeros_like(total)
    for k in range(1, steps_axis):
        other = lax.ppermute(total, "step", xor_pairs(steps_axis, k))
        earlier = earlier + jnp.where((position ^ k) < position, other, zero)
    return earlier[None] + local_cum


def earlier_groups(local_cum, steps_axis):
    every_total = lax.all_gather(local_cum[-1][None], "step", axis=0, tiled=True)
    position = lax.axis_index("step")
    order = jnp.arange(steps_axis, dtype=jnp.int32)
    earlier = jnp.sum(
        jnp.where((order < position)[:, None, None], every_total, jnp.zeros((), jnp.float32)),
        axis=0,
    )
    return earlier[None]


def on_device(
    queries, keys, values, start_latent, out_weight, cfg_table, cfg_index, step_table, time_index
):
    step_dev, branches, heads, tok_dev, head_size = queries.shape
    groups = lax.axis_size("seq")
    steps_axis = lax.axis_size("step")
    items = step_dev * branches * heads
    per_dev = items // groups
    length = tok_dev * groups
    channels = out_weight.shape[0]
    me = lax.axis_index("seq")

    stacked = jnp.stack([queries, keys, values]).reshape(3, groups, per_dev, tok_dev, head_size)
    gathered = lax.all_to_all(stacked, "seq", split_axis=1, concat_axis=3, tiled=True)
    gathered = gathered.reshape(3, per_dev, length, head_size)
    heads_out = attend(gathered[0], gathered[1], gathered[2])

    weight_heads = out_weight.reshape(channels, heads, head_size)
    guide_scale = lookup(cfg_table, cfg_index)[0]
    step_len = lookup(step_table, time_index)

    if per_dev % (branches * heads) == 0:
        local_steps = per_dev // (branches * heads)
        ho = heads_out.reshape(local_steps, branches, heads, length, head_size)
        wide = ho.astype(jnp.float32)
        square_sum = jnp.sum(wide * wide, axis=(2, 4))
        root_mean = jnp.sqrt(square_sum / (H * HD) + 1e-06)
        drift = (
            jnp.einsum("chd,sbhld->sbcl", weight_heads, ho, preferred_element_type=jnp.float32)
            / root_mean[:, :, None, :]
        )
        guided = drift[:, 1] + guide_scale * (drift[:, 0] - drift[:, 1])
        my_len = lax.dynamic_slice_in_dim(step_len, me * local_steps, local_steps)
        update = my_len[:, None, None] * guided
        update = update.reshape(local_steps, channels, groups, tok_dev)
        return start_latent[None] + gather_prefix(update, me, groups, step_dev, steps_axis)

    assert heads % per_dev == 0
    share = heads // per_dev
    first = me * per_dev
    head_ids = (first + jnp.arange(per_dev, dtype=jnp.int32)) % heads
    chosen = jnp.take(weight_heads, head_ids, axis=1)
    numer = jnp.einsum("cid,ild->cl", chosen, heads_out, preferred_element_type=jnp.float32)
    wide = heads_out.astype(jnp.float32)
    square = jnp.sum(wide * wide, axis=(0, 2))
    partial = jnp.concatenate([numer, square[None]], axis=0)
    partial = partial.reshape(channels + 1, groups, tok_dev)
    returned = lax.all_to_all(partial, "seq", split_axis=1, concat_axis=1, tiled=True)
    returned = returned.reshape(channels + 1, step_dev * branches, share, tok_dev)
    summed = jnp.sum(returned, axis=2).reshape(channels + 1, step_dev, branches, tok_dev)
    numer = jnp.transpose(summed[:channels], (1, 2, 0, 3))
    square_sum = summed[channels]
    root_mean = jnp.sqrt(square_sum / (H * HD) + 1e-06)
    drift = numer / root_mean[:, :, None, :]
    guided = drift[:, 1] + guide_scale * (drift[:, 0] - drift[:, 1])
    local_cum = jnp.cumsum(step_len[:, None, None] * guided, axis=0)
    return start_latent[None] + earlier_groups(local_cum, steps_axis) + local_cum


def solution(mesh):
    return jax.shard_map(
        on_device,
        mesh=mesh,
        in_specs=(
            P(("scene", "step"), None, None, "seq", None),
            P(("scene", "step"), None, None, "seq", None),
            P(("scene", "step"), None, None, "seq", None),
            P("scene", "seq"),
            P(),
            P(),
            P("scene"),
            P(),
            P(("scene", "step")),
        ),
        out_specs=P(("scene", "step"), None, "seq"),
        check_vma=False,
    )
```

```python
import jax
import jax.numpy as jnp
from jax import lax
from jax.sharding import PartitionSpec as P

HD = 128
H = 24


def lookup(table, index):
    count = table.shape[0]
    hits = index[..., None] == jnp.arange(count, dtype=jnp.int32)
    return jnp.sum(jnp.where(hits, table, jnp.zeros((), table.dtype)), axis=-1)


def attend(query_rows, key_rows, value_rows):
    scale = HD ** (-0.5)
    scores = (
        jnp.einsum("iqd,ikd->iqk", query_rows, key_rows, preferred_element_type=jnp.float32) * scale
    )
    expo = jnp.exp(scores - jnp.max(scores, axis=-1, keepdims=True))
    total = jnp.sum(expo, axis=-1, keepdims=True)
    weights = expo.astype(jnp.bfloat16)
    out = jnp.einsum("iqk,ikd->iqd", weights, value_rows, preferred_element_type=jnp.float32)
    return (out / total).astype(jnp.bfloat16)


def xor_pairs(size, k):
    return [(i, i ^ k) for i in range(size)]


def gather_prefix(update, me, groups, step_dev, steps_axis):
    local_steps = update.shape[0]
    partners = me ^ jnp.arange(groups, dtype=jnp.int32)
    ordered = jnp.take(update, partners, axis=2)
    pieces = [ordered[:, :, 0]]
    sources = [me]
    for k in range(1, groups):
        pieces.append(lax.ppermute(ordered[:, :, k], "seq", xor_pairs(groups, k)))
        sources.append(me ^ k)
    zero = jnp.zeros((), jnp.float32)
    outs = []
    for s in range(step_dev):
        acc = None
        for piece, source in zip(pieces, sources):
            for t in range(local_steps):
                term = jnp.where(source * local_steps + t <= s, piece[t], zero)
                acc = term if acc is None else acc + term
        outs.append(acc)
    local_cum = jnp.stack(outs)
    total = outs[-1]
    position = lax.axis_index("step")
    earlier = jnp.zeros_like(total)
    for k in range(1, steps_axis):
        other = lax.ppermute(total, "step", xor_pairs(steps_axis, k))
        earlier = earlier + jnp.where((position ^ k) < position, other, zero)
    return earlier[None] + local_cum


def earlier_groups(local_cum, steps_axis):
    every_total = lax.all_gather(local_cum[-1][None], "step", axis=0, tiled=True)
    position = lax.axis_index("step")
    order = jnp.arange(steps_axis, dtype=jnp.int32)
    earlier = jnp.sum(
        jnp.where((order < position)[:, None, None], every_total, jnp.zeros((), jnp.float32)),
        axis=0,
    )
    return earlier[None]


def on_device(
    queries, keys, values, start_latent, out_weight, cfg_table, cfg_index, step_table, time_index
):
    step_dev, branches, heads, tok_dev, head_size = queries.shape
    groups = lax.axis_size("seq")
    steps_axis = lax.axis_size("step")
    items = step_dev * branches * heads
    per_dev = items // groups
    length = tok_dev * groups
    channels = out_weight.shape[0]
    me = lax.axis_index("seq")

    chunks = [a.reshape(groups, per_dev, tok_dev, head_size) for a in (queries, keys, values)]
    stacked = jnp.stack(chunks, axis=1)
    gathered = lax.all_to_all(stacked, "seq", split_axis=0, concat_axis=3, tiled=True)
    gathered = gathered.reshape(3, per_dev, length, head_size)
    heads_out = attend(gathered[0], gathered[1], gathered[2])

    weight_heads = out_weight.reshape(channels, heads, head_size)
    guide_scale = lookup(cfg_table, cfg_index)[0]
    step_len = lookup(step_table, time_index)

    if per_dev % (branches * heads) == 0:
        local_steps = per_dev // (branches * heads)
        ho = heads_out.reshape(local_steps, branches, heads, length, head_size)
        wide = ho.astype(jnp.float32)
        square_sum = jnp.sum(wide * wide, axis=(2, 4))
        root_mean = jnp.sqrt(square_sum / (H * HD) + 1e-06)
        drift = (
            jnp.einsum("chd,sbhld->sbcl", weight_heads, ho, preferred_element_type=jnp.float32)
            / root_mean[:, :, None, :]
        )
        guided = drift[:, 1] + guide_scale * (drift[:, 0] - drift[:, 1])
        my_len = lax.dynamic_slice_in_dim(step_len, me * local_steps, local_steps)
        update = my_len[:, None, None] * guided
        update = update.reshape(local_steps, channels, groups, tok_dev)
        return start_latent[None] + gather_prefix(update, me, groups, step_dev, steps_axis)

    assert heads % per_dev == 0
    share = heads // per_dev
    first = me * per_dev
    head_ids = (first + jnp.arange(per_dev, dtype=jnp.int32)) % heads
    chosen = jnp.take(weight_heads, head_ids, axis=1)
    numer = jnp.einsum("cid,ild->cl", chosen, heads_out, preferred_element_type=jnp.float32)
    wide = heads_out.astype(jnp.float32)
    square = jnp.sum(wide * wide, axis=(0, 2))
    partial = jnp.concatenate([numer, square[None]], axis=0)
    partial = partial.reshape(channels + 1, groups, tok_dev)
    returned = lax.all_to_all(partial, "seq", split_axis=1, concat_axis=1, tiled=True)
    returned = returned.reshape(channels + 1, step_dev * branches, share, tok_dev)
    summed = jnp.sum(returned, axis=2).reshape(channels + 1, step_dev, branches, tok_dev)
    numer = jnp.transpose(summed[:channels], (1, 2, 0, 3))
    square_sum = summed[channels]
    root_mean = jnp.sqrt(square_sum / (H * HD) + 1e-06)
    drift = numer / root_mean[:, :, None, :]
    guided = drift[:, 1] + guide_scale * (drift[:, 0] - drift[:, 1])
    local_cum = jnp.cumsum(step_len[:, None, None] * guided, axis=0)
    return start_latent[None] + earlier_groups(local_cum, steps_axis) + local_cum


def solution(mesh):
    return jax.shard_map(
        on_device,
        mesh=mesh,
        in_specs=(
            P(("scene", "step"), None, None, "seq", None),
            P(("scene", "step"), None, None, "seq", None),
            P(("scene", "step"), None, None, "seq", None),
            P("scene", "seq"),
            P(),
            P(),
            P("scene"),
            P(),
            P(("scene", "step")),
        ),
        out_specs=P(("scene", "step"), None, "seq"),
        check_vma=False,
    )
```

```python
import jax
import jax.numpy as jnp
from jax import lax
from jax.sharding import PartitionSpec as P

HD = 128
H = 24


def lookup(table, index):
    count = table.shape[0]
    hits = index[..., None] == jnp.arange(count, dtype=jnp.int32)
    return jnp.sum(jnp.where(hits, table, jnp.zeros((), table.dtype)), axis=-1)


def attend(query_rows, key_rows, value_rows):
    scale = HD ** (-0.5)
    scores = (
        jnp.einsum("iqd,ikd->iqk", query_rows, key_rows, preferred_element_type=jnp.float32) * scale
    )
    expo = jnp.exp(scores - jnp.max(scores, axis=-1, keepdims=True))
    total = jnp.sum(expo, axis=-1, keepdims=True)
    weights = expo.astype(jnp.bfloat16)
    out = jnp.einsum("iqk,ikd->iqd", weights, value_rows, preferred_element_type=jnp.float32)
    return (out / total).astype(jnp.bfloat16)


def xor_pairs(size, k):
    return [(i, i ^ k) for i in range(size)]


def gather_prefix(update, me, groups, step_dev, steps_axis, partner_order):
    local_steps = update.shape[0]
    if partner_order:
        ordered = update
    else:
        partners = me ^ jnp.arange(groups, dtype=jnp.int32)
        ordered = jnp.take(update, partners, axis=2)
    pieces = [ordered[:, :, 0]]
    sources = [me]
    for k in range(1, groups):
        pieces.append(lax.ppermute(ordered[:, :, k], "seq", xor_pairs(groups, k)))
        sources.append(me ^ k)
    zero = jnp.zeros((), jnp.float32)
    outs = []
    for s in range(step_dev):
        acc = None
        for piece, source in zip(pieces, sources):
            for t in range(local_steps):
                term = jnp.where(source * local_steps + t <= s, piece[t], zero)
                acc = term if acc is None else acc + term
        outs.append(acc)
    local_cum = jnp.stack(outs)
    total = outs[-1]
    position = lax.axis_index("step")
    earlier = jnp.zeros_like(total)
    for k in range(1, steps_axis):
        other = lax.ppermute(total, "step", xor_pairs(steps_axis, k))
        earlier = earlier + jnp.where((position ^ k) < position, other, zero)
    return earlier[None] + local_cum


def earlier_groups(local_cum, steps_axis):
    every_total = lax.all_gather(local_cum[-1][None], "step", axis=0, tiled=True)
    position = lax.axis_index("step")
    order = jnp.arange(steps_axis, dtype=jnp.int32)
    earlier = jnp.sum(
        jnp.where((order < position)[:, None, None], every_total, jnp.zeros((), jnp.float32)),
        axis=0,
    )
    return earlier[None]


def on_device(
    queries, keys, values, start_latent, out_weight, cfg_table, cfg_index, step_table, time_index
):
    step_dev, branches, heads, tok_dev, head_size = queries.shape
    groups = lax.axis_size("seq")
    steps_axis = lax.axis_size("step")
    items = step_dev * branches * heads
    per_dev = items // groups
    length = tok_dev * groups
    channels = out_weight.shape[0]
    me = lax.axis_index("seq")

    chunks = [a.reshape(groups, per_dev, tok_dev, head_size) for a in (queries, keys, values)]
    whole_steps = per_dev % (branches * heads) == 0
    if whole_steps and groups & (groups - 1) == 0:
        arrived = []
        for k in range(groups):
            piece = jnp.stack(
                [lax.dynamic_index_in_dim(c, me ^ k, 0, keepdims=False) for c in chunks]
            )
            if k:
                piece = lax.ppermute(piece, "seq", xor_pairs(groups, k))
            arrived.append(piece)
        gathered = jnp.concatenate(arrived, axis=2)
        partner_order = True
    else:
        stacked = jnp.stack(chunks, axis=1)
        gathered = lax.all_to_all(stacked, "seq", split_axis=0, concat_axis=3, tiled=True)
        gathered = gathered.reshape(3, per_dev, length, head_size)
        partner_order = False
    heads_out = attend(gathered[0], gathered[1], gathered[2])

    weight_heads = out_weight.reshape(channels, heads, head_size)
    guide_scale = lookup(cfg_table, cfg_index)[0]
    step_len = lookup(step_table, time_index)

    if whole_steps:
        local_steps = per_dev // (branches * heads)
        ho = heads_out.reshape(local_steps, branches, heads, length, head_size)
        wide = ho.astype(jnp.float32)
        square_sum = jnp.sum(wide * wide, axis=(2, 4))
        root_mean = jnp.sqrt(square_sum / (H * HD) + 1e-06)
        drift = (
            jnp.einsum("chd,sbhld->sbcl", weight_heads, ho, preferred_element_type=jnp.float32)
            / root_mean[:, :, None, :]
        )
        guided = drift[:, 1] + guide_scale * (drift[:, 0] - drift[:, 1])
        my_len = lax.dynamic_slice_in_dim(step_len, me * local_steps, local_steps)
        update = my_len[:, None, None] * guided
        update = update.reshape(local_steps, channels, groups, tok_dev)
        return start_latent[None] + gather_prefix(
            update, me, groups, step_dev, steps_axis, partner_order
        )

    assert heads % per_dev == 0
    share = heads // per_dev
    first = me * per_dev
    head_ids = (first + jnp.arange(per_dev, dtype=jnp.int32)) % heads
    chosen = jnp.take(weight_heads, head_ids, axis=1)
    numer = jnp.einsum("cid,ild->cl", chosen, heads_out, preferred_element_type=jnp.float32)
    wide = heads_out.astype(jnp.float32)
    square = jnp.sum(wide * wide, axis=(0, 2))
    partial = jnp.concatenate([numer, square[None]], axis=0)
    partial = partial.reshape(channels + 1, groups, tok_dev)
    returned = lax.all_to_all(partial, "seq", split_axis=1, concat_axis=1, tiled=True)
    returned = returned.reshape(channels + 1, step_dev * branches, share, tok_dev)
    summed = jnp.sum(returned, axis=2).reshape(channels + 1, step_dev, branches, tok_dev)
    numer = jnp.transpose(summed[:channels], (1, 2, 0, 3))
    square_sum = summed[channels]
    root_mean = jnp.sqrt(square_sum / (H * HD) + 1e-06)
    drift = numer / root_mean[:, :, None, :]
    guided = drift[:, 1] + guide_scale * (drift[:, 0] - drift[:, 1])
    local_cum = jnp.cumsum(step_len[:, None, None] * guided, axis=0)
    return start_latent[None] + earlier_groups(local_cum, steps_axis) + local_cum


def solution(mesh):
    return jax.shard_map(
        on_device,
        mesh=mesh,
        in_specs=(
            P(("scene", "step"), None, None, "seq", None),
            P(("scene", "step"), None, None, "seq", None),
            P(("scene", "step"), None, None, "seq", None),
            P("scene", "seq"),
            P(),
            P(),
            P("scene"),
            P(),
            P(("scene", "step")),
        ),
        out_specs=P(("scene", "step"), None, "seq"),
        check_vma=False,
    )
```

```python
import jax
import jax.numpy as jnp
from jax import lax
from jax.sharding import PartitionSpec as P

HD = 128
H = 24


def lookup(table, index):
    count = table.shape[0]
    hits = index[..., None] == jnp.arange(count, dtype=jnp.int32)
    return jnp.sum(jnp.where(hits, table, jnp.zeros((), table.dtype)), axis=-1)


def attend(query_rows, key_rows, value_rows):
    scale = HD ** (-0.5)
    scores = (
        jnp.einsum("iqd,ikd->iqk", query_rows, key_rows, preferred_element_type=jnp.float32) * scale
    )
    expo = jnp.exp(scores - jnp.max(scores, axis=-1, keepdims=True))
    total = jnp.sum(expo, axis=-1, keepdims=True)
    weights = expo.astype(jnp.bfloat16)
    out = jnp.einsum("iqk,ikd->iqd", weights, value_rows, preferred_element_type=jnp.float32)
    return (out / total).astype(jnp.bfloat16)


def xor_pairs(size, k):
    return [(i, i ^ k) for i in range(size)]


def gather_prefix(update, me, groups, step_dev, steps_axis, partner_order):
    local_steps = update.shape[0]
    if partner_order:
        ordered = update
    else:
        partners = me ^ jnp.arange(groups, dtype=jnp.int32)
        ordered = jnp.take(update, partners, axis=2)
    pieces = [ordered[:, :, 0]]
    sources = [me]
    for k in range(1, groups):
        pieces.append(lax.ppermute(ordered[:, :, k], "seq", xor_pairs(groups, k)))
        sources.append(me ^ k)
    zero = jnp.zeros((), jnp.float32)
    outs = []
    for s in range(step_dev):
        acc = None
        for piece, source in zip(pieces, sources):
            for t in range(local_steps):
                term = jnp.where(source * local_steps + t <= s, piece[t], zero)
                acc = term if acc is None else acc + term
        outs.append(acc)
    local_cum = jnp.stack(outs)
    total = outs[-1]
    position = lax.axis_index("step")
    earlier = jnp.zeros_like(total)
    for k in range(1, steps_axis):
        other = lax.ppermute(total, "step", xor_pairs(steps_axis, k))
        earlier = earlier + jnp.where((position ^ k) < position, other, zero)
    return earlier[None] + local_cum


def earlier_groups(local_cum, steps_axis):
    every_total = lax.all_gather(local_cum[-1][None], "step", axis=0, tiled=True)
    position = lax.axis_index("step")
    order = jnp.arange(steps_axis, dtype=jnp.int32)
    earlier = jnp.sum(
        jnp.where((order < position)[:, None, None], every_total, jnp.zeros((), jnp.float32)),
        axis=0,
    )
    return earlier[None]


def on_device(
    queries, keys, values, start_latent, out_weight, cfg_table, cfg_index, step_table, time_index
):
    step_dev, branches, heads, tok_dev, head_size = queries.shape
    groups = lax.axis_size("seq")
    steps_axis = lax.axis_size("step")
    items = step_dev * branches * heads
    per_dev = items // groups
    length = tok_dev * groups
    channels = out_weight.shape[0]
    me = lax.axis_index("seq")

    chunks = [a.reshape(groups, per_dev, tok_dev, head_size) for a in (queries, keys, values)]
    whole_steps = per_dev % (branches * heads) == 0
    if whole_steps and groups & (groups - 1) == 0:
        arrived = {}
        for k in reversed(range(groups)):
            pieces = [lax.dynamic_index_in_dim(c, me ^ k, 0, keepdims=False) for c in chunks]
            if k:
                pieces = [lax.ppermute(p, "seq", xor_pairs(groups, k)) for p in pieces]
            arrived[k] = pieces
        gathered = [
            jnp.concatenate([arrived[k][i] for k in range(groups)], axis=1) for i in range(3)
        ]
        partner_order = True
    else:
        stacked = jnp.stack(chunks, axis=1)
        gathered = lax.all_to_all(stacked, "seq", split_axis=0, concat_axis=3, tiled=True)
        gathered = gathered.reshape(3, per_dev, length, head_size)
        partner_order = False
    heads_out = attend(gathered[0], gathered[1], gathered[2])

    weight_heads = out_weight.reshape(channels, heads, head_size)
    guide_scale = lookup(cfg_table, cfg_index)[0]
    step_len = lookup(step_table, time_index)

    if whole_steps:
        local_steps = per_dev // (branches * heads)
        ho = heads_out.reshape(local_steps, branches, heads, length, head_size)
        wide = ho.astype(jnp.float32)
        square_sum = jnp.sum(wide * wide, axis=(2, 4))
        root_mean = jnp.sqrt(square_sum / (H * HD) + 1e-06)
        drift = (
            jnp.einsum("chd,sbhld->sbcl", weight_heads, ho, preferred_element_type=jnp.float32)
            / root_mean[:, :, None, :]
        )
        guided = drift[:, 1] + guide_scale * (drift[:, 0] - drift[:, 1])
        my_len = lax.dynamic_slice_in_dim(step_len, me * local_steps, local_steps)
        update = my_len[:, None, None] * guided
        update = update.reshape(local_steps, channels, groups, tok_dev)
        return start_latent[None] + gather_prefix(
            update, me, groups, step_dev, steps_axis, partner_order
        )

    assert heads % per_dev == 0
    share = heads // per_dev
    first = me * per_dev
    head_ids = (first + jnp.arange(per_dev, dtype=jnp.int32)) % heads
    chosen = jnp.take(weight_heads, head_ids, axis=1)
    numer = jnp.einsum("cid,ild->cl", chosen, heads_out, preferred_element_type=jnp.float32)
    wide = heads_out.astype(jnp.float32)
    square = jnp.sum(wide * wide, axis=(0, 2))
    partial = jnp.concatenate([numer, square[None]], axis=0)
    partial = partial.reshape(channels + 1, groups, tok_dev)
    returned = lax.all_to_all(partial, "seq", split_axis=1, concat_axis=1, tiled=True)
    returned = returned.reshape(channels + 1, step_dev * branches, share, tok_dev)
    summed = jnp.sum(returned, axis=2).reshape(channels + 1, step_dev, branches, tok_dev)
    numer = jnp.transpose(summed[:channels], (1, 2, 0, 3))
    square_sum = summed[channels]
    root_mean = jnp.sqrt(square_sum / (H * HD) + 1e-06)
    drift = numer / root_mean[:, :, None, :]
    guided = drift[:, 1] + guide_scale * (drift[:, 0] - drift[:, 1])
    local_cum = jnp.cumsum(step_len[:, None, None] * guided, axis=0)
    return start_latent[None] + earlier_groups(local_cum, steps_axis) + local_cum


def solution(mesh):
    return jax.shard_map(
        on_device,
        mesh=mesh,
        in_specs=(
            P(("scene", "step"), None, None, "seq", None),
            P(("scene", "step"), None, None, "seq", None),
            P(("scene", "step"), None, None, "seq", None),
            P("scene", "seq"),
            P(),
            P(),
            P("scene"),
            P(),
            P(("scene", "step")),
        ),
        out_specs=P(("scene", "step"), None, "seq"),
        check_vma=False,
    )
```

```python
import jax
import jax.numpy as jnp
from jax import lax
from jax.sharding import PartitionSpec as P

HD = 128
H = 24


def lookup(table, index):
    count = table.shape[0]
    hits = index[..., None] == jnp.arange(count, dtype=jnp.int32)
    return jnp.sum(jnp.where(hits, table, jnp.zeros((), table.dtype)), axis=-1)


def attend(query_rows, key_rows, value_rows):
    scale = HD ** (-0.5)
    scores = (
        jnp.einsum("iqd,ikd->iqk", query_rows, key_rows, preferred_element_type=jnp.float32) * scale
    )
    expo = jnp.exp(scores - jnp.max(scores, axis=-1, keepdims=True))
    total = jnp.sum(expo, axis=-1, keepdims=True)
    weights = expo.astype(jnp.bfloat16)
    out = jnp.einsum("iqk,ikd->iqd", weights, value_rows, preferred_element_type=jnp.float32)
    return (out / total).astype(jnp.bfloat16)


def xor_pairs(size, k):
    return [(i, i ^ k) for i in range(size)]


def gather_prefix(update, start, me, groups, step_dev, steps_axis, partner_order):
    local_steps = update.shape[0]
    if partner_order:
        ordered = update
    else:
        partners = me ^ jnp.arange(groups, dtype=jnp.int32)
        ordered = jnp.take(update, partners, axis=1)
    pieces = [ordered[:, 0]]
    sources = [me]
    for k in range(1, groups):
        pieces.append(lax.ppermute(ordered[:, k], "seq", xor_pairs(groups, k)))
        sources.append(me ^ k)
    zero = jnp.zeros((), jnp.float32)
    outs = []
    for s in range(step_dev):
        acc = None
        for piece, source in zip(pieces, sources):
            for t in range(local_steps):
                term = jnp.where(source * local_steps + t <= s, piece[t], zero)
                acc = term if acc is None else acc + term
        outs.append(acc)
    total = outs[-1]
    local_cum = jnp.stack(outs) + start[None]
    position = lax.axis_index("step")
    earlier = jnp.zeros_like(total)
    for k in range(1, steps_axis):
        other = lax.ppermute(total, "step", xor_pairs(steps_axis, k))
        earlier = earlier + jnp.where((position ^ k) < position, other, zero)
    return jnp.transpose(local_cum + earlier[None], (0, 2, 1))


def earlier_groups(local_cum, steps_axis):
    every_total = lax.all_gather(local_cum[-1][None], "step", axis=0, tiled=True)
    position = lax.axis_index("step")
    order = jnp.arange(steps_axis, dtype=jnp.int32)
    earlier = jnp.sum(
        jnp.where((order < position)[:, None, None], every_total, jnp.zeros((), jnp.float32)),
        axis=0,
    )
    return earlier[None]


def on_device(
    queries, keys, values, start_latent, out_weight, cfg_table, cfg_index, step_table, time_index
):
    step_dev, branches, heads, tok_dev, head_size = queries.shape
    groups = lax.axis_size("seq")
    steps_axis = lax.axis_size("step")
    items = step_dev * branches * heads
    per_dev = items // groups
    length = tok_dev * groups
    channels = out_weight.shape[0]
    me = lax.axis_index("seq")

    chunks = [a.reshape(groups, per_dev, tok_dev, head_size) for a in (queries, keys, values)]
    whole_steps = per_dev % (branches * heads) == 0
    if whole_steps and groups & (groups - 1) == 0:
        arrived = {}
        for k in reversed(range(groups)):
            pieces = [lax.dynamic_index_in_dim(c, me ^ k, 0, keepdims=False) for c in chunks]
            if k:
                pieces = [lax.ppermute(p, "seq", xor_pairs(groups, k)) for p in pieces]
            arrived[k] = pieces
        gathered = [
            jnp.concatenate([arrived[k][i] for k in range(groups)], axis=1) for i in range(3)
        ]
        partner_order = True
    else:
        stacked = jnp.stack(chunks, axis=1)
        gathered = lax.all_to_all(stacked, "seq", split_axis=0, concat_axis=3, tiled=True)
        gathered = gathered.reshape(3, per_dev, length, head_size)
        partner_order = False
    heads_out = attend(gathered[0], gathered[1], gathered[2])

    weight_heads = out_weight.reshape(channels, heads, head_size)
    guide_scale = lookup(cfg_table, cfg_index)[0]
    step_len = lookup(step_table, time_index)

    if whole_steps:
        local_steps = per_dev // (branches * heads)
        ho = heads_out.reshape(local_steps, branches, heads, length, head_size)
        wide = ho.astype(jnp.float32)
        square_sum = jnp.sum(wide * wide, axis=(2, 4))
        root_mean = jnp.sqrt(square_sum / (H * HD) + 1e-06)
        drift = (
            jnp.einsum("chd,sbhld->sblc", weight_heads, ho, preferred_element_type=jnp.float32)
            / root_mean[:, :, :, None]
        )
        guided = drift[:, 1] + guide_scale * (drift[:, 0] - drift[:, 1])
        my_len = lax.dynamic_slice_in_dim(step_len, me * local_steps, local_steps)
        update = my_len[:, None, None] * guided
        update = update.reshape(local_steps, groups, tok_dev, channels)
        return gather_prefix(
            update, start_latent.T, me, groups, step_dev, steps_axis, partner_order
        )

    assert heads % per_dev == 0
    share = heads // per_dev
    first = me * per_dev
    head_ids = (first + jnp.arange(per_dev, dtype=jnp.int32)) % heads
    chosen = jnp.take(weight_heads, head_ids, axis=1)
    numer = jnp.einsum("cid,ild->cl", chosen, heads_out, preferred_element_type=jnp.float32)
    wide = heads_out.astype(jnp.float32)
    square = jnp.sum(wide * wide, axis=(0, 2))
    partial = jnp.concatenate([numer, square[None]], axis=0)
    partial = partial.reshape(channels + 1, groups, tok_dev)
    returned = lax.all_to_all(partial, "seq", split_axis=1, concat_axis=1, tiled=True)
    returned = returned.reshape(channels + 1, step_dev * branches, share, tok_dev)
    summed = jnp.sum(returned, axis=2).reshape(channels + 1, step_dev, branches, tok_dev)
    numer = jnp.transpose(summed[:channels], (1, 2, 0, 3))
    square_sum = summed[channels]
    root_mean = jnp.sqrt(square_sum / (H * HD) + 1e-06)
    drift = numer / root_mean[:, :, None, :]
    guided = drift[:, 1] + guide_scale * (drift[:, 0] - drift[:, 1])
    local_cum = jnp.cumsum(step_len[:, None, None] * guided, axis=0)
    return start_latent[None] + earlier_groups(local_cum, steps_axis) + local_cum


def solution(mesh):
    return jax.shard_map(
        on_device,
        mesh=mesh,
        in_specs=(
            P(("scene", "step"), None, None, "seq", None),
            P(("scene", "step"), None, None, "seq", None),
            P(("scene", "step"), None, None, "seq", None),
            P("scene", "seq"),
            P(),
            P(),
            P("scene"),
            P(),
            P(("scene", "step")),
        ),
        out_specs=P(("scene", "step"), None, "seq"),
        check_vma=False,
    )
```

```python
import jax
import jax.numpy as jnp
from jax import lax
from jax.sharding import PartitionSpec as P

HD = 128
H = 24


def lookup(table, index):
    count = table.shape[0]
    hits = index[..., None] == jnp.arange(count, dtype=jnp.int32)
    return jnp.sum(jnp.where(hits, table, jnp.zeros((), table.dtype)), axis=-1)


def attend(query_rows, key_rows, value_rows):
    scale = HD ** (-0.5)
    scores = (
        jnp.einsum("iqd,ikd->iqk", query_rows, key_rows, preferred_element_type=jnp.float32) * scale
    )
    expo = jnp.exp(scores - jnp.max(scores, axis=-1, keepdims=True))
    total = jnp.sum(expo, axis=-1, keepdims=True)
    weights = expo.astype(jnp.bfloat16)
    out = jnp.einsum("iqk,ikd->iqd", weights, value_rows, preferred_element_type=jnp.float32)
    return (out / total).astype(jnp.bfloat16)


def xor_pairs(size, k):
    return [(i, i ^ k) for i in range(size)]


def gather_prefix(update, start, me, groups, step_dev, steps_axis, partner_order):
    local_steps = update.shape[0]
    if partner_order:
        ordered = update
    else:
        partners = me ^ jnp.arange(groups, dtype=jnp.int32)
        ordered = jnp.take(update, partners, axis=1)
    pieces = [ordered[:, 0]]
    sources = [me]
    for k in range(1, groups):
        pieces.append(lax.ppermute(ordered[:, k], "seq", xor_pairs(groups, k)))
        sources.append(me ^ k)
    zero = jnp.zeros((), jnp.float32)
    outs = []
    for s in range(step_dev):
        acc = None
        for piece, source in zip(pieces, sources):
            for t in range(local_steps):
                term = jnp.where(source * local_steps + t <= s, piece[t], zero)
                acc = term if acc is None else acc + term
        outs.append(acc)
    total = outs[-1]
    local_cum = jnp.stack(outs) + start[None]
    position = lax.axis_index("step")
    earlier = jnp.zeros_like(total)
    for k in range(1, steps_axis):
        other = lax.ppermute(total, "step", xor_pairs(steps_axis, k))
        earlier = earlier + jnp.where((position ^ k) < position, other, zero)
    return jnp.transpose(local_cum + earlier[None], (0, 2, 1))


def earlier_groups(local_cum, steps_axis):
    every_total = lax.all_gather(local_cum[-1][None], "step", axis=0, tiled=True)
    position = lax.axis_index("step")
    order = jnp.arange(steps_axis, dtype=jnp.int32)
    earlier = jnp.sum(
        jnp.where((order < position)[:, None, None], every_total, jnp.zeros((), jnp.float32)),
        axis=0,
    )
    return earlier[None]


def on_device(
    queries, keys, values, start_latent, out_weight, cfg_table, cfg_index, step_table, time_index
):
    step_dev, branches, heads, tok_dev, head_size = queries.shape
    groups = lax.axis_size("seq")
    steps_axis = lax.axis_size("step")
    items = step_dev * branches * heads
    per_dev = items // groups
    length = tok_dev * groups
    channels = out_weight.shape[0]
    me = lax.axis_index("seq")

    chunks = [a.reshape(groups, per_dev, tok_dev, head_size) for a in (queries, keys, values)]
    whole_steps = per_dev % (branches * heads) == 0
    if whole_steps and groups & (groups - 1) == 0:
        arrived = {}
        for k in reversed(range(groups)):
            pieces = [lax.dynamic_index_in_dim(c, me ^ k, 0, keepdims=False) for c in chunks]
            if k:
                pieces = [lax.ppermute(p, "seq", xor_pairs(groups, k)) for p in pieces]
            arrived[k] = pieces
        gathered = [
            jnp.concatenate([arrived[k][i] for k in range(groups)], axis=1) for i in range(3)
        ]
        partner_order = True
    else:
        stacked = jnp.stack(chunks, axis=1)
        gathered = lax.all_to_all(stacked, "seq", split_axis=0, concat_axis=3, tiled=True)
        gathered = gathered.reshape(3, per_dev, length, head_size)
        partner_order = False
    heads_out = attend(gathered[0], gathered[1], gathered[2])

    weight_heads = out_weight.reshape(channels, heads, head_size)
    guide_scale = lookup(cfg_table, cfg_index)[0]
    step_len = lookup(step_table, time_index)

    if whole_steps:
        local_steps = per_dev // (branches * heads)
        ho = heads_out.reshape(local_steps, branches, heads, length, head_size)
        wide = ho.astype(jnp.float32)
        square_sum = jnp.sum(wide * wide, axis=(2, 4))
        root_mean = jnp.sqrt(square_sum / (H * HD) + 1e-06)
        drift = (
            jnp.einsum("chd,sbhld->sblc", weight_heads, ho, preferred_element_type=jnp.float32)
            / root_mean[:, :, :, None]
        )
        my_len = lax.dynamic_slice_in_dim(step_len, me * local_steps, local_steps)
        shape = (local_steps, length, channels)
        scale_full, len_full = lax.optimization_barrier(
            (
                jnp.broadcast_to(guide_scale, shape),
                jnp.broadcast_to(my_len[:, None, None], shape),
            )
        )
        guided = drift[:, 1] + scale_full * (drift[:, 0] - drift[:, 1])
        update = len_full * guided
        update = update.reshape(local_steps, groups, tok_dev, channels)
        return gather_prefix(
            update, start_latent.T, me, groups, step_dev, steps_axis, partner_order
        )

    assert heads % per_dev == 0
    share = heads // per_dev
    first = me * per_dev
    head_ids = (first + jnp.arange(per_dev, dtype=jnp.int32)) % heads
    chosen = jnp.take(weight_heads, head_ids, axis=1)
    numer = jnp.einsum("cid,ild->cl", chosen, heads_out, preferred_element_type=jnp.float32)
    wide = heads_out.astype(jnp.float32)
    square = jnp.sum(wide * wide, axis=(0, 2))
    partial = jnp.concatenate([numer, square[None]], axis=0)
    partial = partial.reshape(channels + 1, groups, tok_dev)
    returned = lax.all_to_all(partial, "seq", split_axis=1, concat_axis=1, tiled=True)
    returned = returned.reshape(channels + 1, step_dev * branches, share, tok_dev)
    summed = jnp.sum(returned, axis=2).reshape(channels + 1, step_dev, branches, tok_dev)
    numer = jnp.transpose(summed[:channels], (1, 2, 0, 3))
    square_sum = summed[channels]
    root_mean = jnp.sqrt(square_sum / (H * HD) + 1e-06)
    drift = numer / root_mean[:, :, None, :]
    guided = drift[:, 1] + guide_scale * (drift[:, 0] - drift[:, 1])
    local_cum = jnp.cumsum(step_len[:, None, None] * guided, axis=0)
    return start_latent[None] + earlier_groups(local_cum, steps_axis) + local_cum


def solution(mesh):
    return jax.shard_map(
        on_device,
        mesh=mesh,
        in_specs=(
            P(("scene", "step"), None, None, "seq", None),
            P(("scene", "step"), None, None, "seq", None),
            P(("scene", "step"), None, None, "seq", None),
            P("scene", "seq"),
            P(),
            P(),
            P("scene"),
            P(),
            P(("scene", "step")),
        ),
        out_specs=P(("scene", "step"), None, "seq"),
        check_vma=False,
    )
```

```python
import jax
import jax.numpy as jnp
from jax import lax
from jax.sharding import PartitionSpec as P

HD = 128
H = 24


def lookup(table, index):
    count = table.shape[0]
    hits = index[..., None] == jnp.arange(count, dtype=jnp.int32)
    return jnp.sum(jnp.where(hits, table, jnp.zeros((), table.dtype)), axis=-1)


def attend(query_rows, key_rows, value_rows):
    scale = HD ** (-0.5)
    scores = (
        jnp.einsum("iqd,ikd->iqk", query_rows, key_rows, preferred_element_type=jnp.float32) * scale
    )
    expo = jnp.exp(scores - jnp.max(scores, axis=-1, keepdims=True))
    total = jnp.sum(expo, axis=-1, keepdims=True)
    weights = expo.astype(jnp.bfloat16)
    out = jnp.einsum("iqk,ikd->iqd", weights, value_rows, preferred_element_type=jnp.float32)
    return (out / total).astype(jnp.bfloat16)


def xor_pairs(size, k):
    return [(i, i ^ k) for i in range(size)]


def gather_prefix(update, start, me, groups, step_dev, steps_axis, partner_order):
    local_steps = update.shape[0]
    if partner_order:
        ordered = update
    else:
        partners = me ^ jnp.arange(groups, dtype=jnp.int32)
        ordered = jnp.take(update, partners, axis=1)
    pieces = [ordered[:, 0]]
    sources = [me]
    for k in range(1, groups):
        pieces.append(lax.ppermute(ordered[:, k], "seq", xor_pairs(groups, k)))
        sources.append(me ^ k)
    zero = jnp.zeros((), jnp.float32)
    outs = []
    for s in range(step_dev):
        acc = None
        for piece, source in zip(pieces, sources):
            for t in range(local_steps):
                term = jnp.where(source * local_steps + t <= s, piece[t], zero)
                acc = term if acc is None else acc + term
        outs.append(acc)
    total = outs[-1]
    local_cum = lax.optimization_barrier(jnp.stack(outs) + start[None])
    position = lax.axis_index("step")
    earlier = jnp.zeros_like(total)
    for k in range(1, steps_axis):
        other = lax.ppermute(total, "step", xor_pairs(steps_axis, k))
        earlier = earlier + jnp.where((position ^ k) < position, other, zero)
    return jnp.transpose(local_cum + earlier[None], (0, 2, 1))


def earlier_groups(local_cum, steps_axis):
    every_total = lax.all_gather(local_cum[-1][None], "step", axis=0, tiled=True)
    position = lax.axis_index("step")
    order = jnp.arange(steps_axis, dtype=jnp.int32)
    earlier = jnp.sum(
        jnp.where((order < position)[:, None, None], every_total, jnp.zeros((), jnp.float32)),
        axis=0,
    )
    return earlier[None]


def on_device(
    queries, keys, values, start_latent, out_weight, cfg_table, cfg_index, step_table, time_index
):
    step_dev, branches, heads, tok_dev, head_size = queries.shape
    groups = lax.axis_size("seq")
    steps_axis = lax.axis_size("step")
    items = step_dev * branches * heads
    per_dev = items // groups
    length = tok_dev * groups
    channels = out_weight.shape[0]
    me = lax.axis_index("seq")

    chunks = [a.reshape(groups, per_dev, tok_dev, head_size) for a in (queries, keys, values)]
    whole_steps = per_dev % (branches * heads) == 0
    if whole_steps and groups & (groups - 1) == 0:
        arrived = {}
        for k in reversed(range(groups)):
            pieces = [lax.dynamic_index_in_dim(c, me ^ k, 0, keepdims=False) for c in chunks]
            if k:
                pieces = [lax.ppermute(p, "seq", xor_pairs(groups, k)) for p in pieces]
            arrived[k] = pieces
        gathered = [
            jnp.concatenate([arrived[k][i] for k in range(groups)], axis=1) for i in range(3)
        ]
        partner_order = True
    else:
        stacked = jnp.stack(chunks, axis=1)
        gathered = lax.all_to_all(stacked, "seq", split_axis=0, concat_axis=3, tiled=True)
        gathered = gathered.reshape(3, per_dev, length, head_size)
        partner_order = False
    heads_out = attend(gathered[0], gathered[1], gathered[2])

    weight_heads = out_weight.reshape(channels, heads, head_size)
    guide_scale = lookup(cfg_table, cfg_index)[0]
    step_len = lookup(step_table, time_index)

    if whole_steps:
        local_steps = per_dev // (branches * heads)
        ho = heads_out.reshape(local_steps, branches, heads, length, head_size)
        wide = ho.astype(jnp.float32)
        square_sum = jnp.sum(wide * wide, axis=(2, 4))
        root_mean = jnp.sqrt(square_sum / (H * HD) + 1e-06)
        drift = (
            jnp.einsum("chd,sbhld->sblc", weight_heads, ho, preferred_element_type=jnp.float32)
            / root_mean[:, :, :, None]
        )
        my_len = lax.dynamic_slice_in_dim(step_len, me * local_steps, local_steps)
        shape = (local_steps, length, channels)
        scale_full, len_full, start_t = lax.optimization_barrier(
            (
                jnp.broadcast_to(guide_scale, shape),
                jnp.broadcast_to(my_len[:, None, None], shape),
                start_latent.T,
            )
        )
        guided = drift[:, 1] + scale_full * (drift[:, 0] - drift[:, 1])
        update = len_full * guided
        update = update.reshape(local_steps, groups, tok_dev, channels)
        return gather_prefix(
            update, start_t, me, groups, step_dev, steps_axis, partner_order
        )

    assert heads % per_dev == 0
    share = heads // per_dev
    first = me * per_dev
    head_ids = (first + jnp.arange(per_dev, dtype=jnp.int32)) % heads
    chosen = jnp.take(weight_heads, head_ids, axis=1)
    numer = jnp.einsum("cid,ild->cl", chosen, heads_out, preferred_element_type=jnp.float32)
    wide = heads_out.astype(jnp.float32)
    square = jnp.sum(wide * wide, axis=(0, 2))
    partial = jnp.concatenate([numer, square[None]], axis=0)
    partial = partial.reshape(channels + 1, groups, tok_dev)
    returned = lax.all_to_all(partial, "seq", split_axis=1, concat_axis=1, tiled=True)
    returned = returned.reshape(channels + 1, step_dev * branches, share, tok_dev)
    summed = jnp.sum(returned, axis=2).reshape(channels + 1, step_dev, branches, tok_dev)
    numer = jnp.transpose(summed[:channels], (1, 2, 0, 3))
    square_sum = summed[channels]
    root_mean = jnp.sqrt(square_sum / (H * HD) + 1e-06)
    drift = numer / root_mean[:, :, None, :]
    guided = drift[:, 1] + guide_scale * (drift[:, 0] - drift[:, 1])
    local_cum = jnp.cumsum(step_len[:, None, None] * guided, axis=0)
    return start_latent[None] + earlier_groups(local_cum, steps_axis) + local_cum


def solution(mesh):
    return jax.shard_map(
        on_device,
        mesh=mesh,
        in_specs=(
            P(("scene", "step"), None, None, "seq", None),
            P(("scene", "step"), None, None, "seq", None),
            P(("scene", "step"), None, None, "seq", None),
            P("scene", "seq"),
            P(),
            P(),
            P("scene"),
            P(),
            P(("scene", "step")),
        ),
        out_specs=P(("scene", "step"), None, "seq"),
        check_vma=False,
    )
```

```python
import jax
import jax.numpy as jnp
from jax import lax
from jax.sharding import PartitionSpec as P

HD = 128
H = 24


def lookup(table, index):
    count = table.shape[0]
    hits = index[..., None] == jnp.arange(count, dtype=jnp.int32)
    return jnp.sum(jnp.where(hits, table, jnp.zeros((), table.dtype)), axis=-1)


def attend(query_rows, key_rows, value_rows):
    scale = HD ** (-0.5)
    scores = (
        jnp.einsum("iqd,ikd->iqk", query_rows, key_rows, preferred_element_type=jnp.float32) * scale
    )
    expo = jnp.exp(scores - jnp.max(scores, axis=-1, keepdims=True))
    total = jnp.sum(expo, axis=-1, keepdims=True)
    weights = expo.astype(jnp.bfloat16)
    out = jnp.einsum("iqk,ikd->iqd", weights, value_rows, preferred_element_type=jnp.float32)
    return (out / total).astype(jnp.bfloat16)


def xor_pairs(size, k):
    return [(i, i ^ k) for i in range(size)]


def gather_prefix(update, start, me, groups, step_dev, steps_axis, partner_order):
    local_steps = update.shape[0]
    if partner_order:
        ordered = update
    else:
        partners = me ^ jnp.arange(groups, dtype=jnp.int32)
        ordered = jnp.take(update, partners, axis=1)
    pieces = [ordered[:, 0]]
    sources = [me]
    for k in range(1, groups):
        pieces.append(lax.ppermute(ordered[:, k], "seq", xor_pairs(groups, k)))
        sources.append(me ^ k)
    zero = jnp.zeros((), jnp.float32)
    outs = []
    for s in range(step_dev):
        acc = None
        for piece, source in zip(pieces, sources):
            for t in range(local_steps):
                term = jnp.where(source * local_steps + t <= s, piece[t], zero)
                acc = term if acc is None else acc + term
        outs.append(acc)
    total = outs[-1]
    local_cum = lax.optimization_barrier(jnp.stack(outs) + start[None])
    position = lax.axis_index("step")
    earlier = jnp.zeros_like(total)
    for k in range(1, steps_axis):
        other = lax.ppermute(total, "step", xor_pairs(steps_axis, k))
        earlier = earlier + jnp.where((position ^ k) < position, other, zero)
    return jnp.transpose(local_cum + earlier[None], (0, 2, 1))


def earlier_groups(local_cum, steps_axis):
    every_total = lax.all_gather(local_cum[-1][None], "step", axis=0, tiled=True)
    position = lax.axis_index("step")
    order = jnp.arange(steps_axis, dtype=jnp.int32)
    earlier = jnp.sum(
        jnp.where((order < position)[:, None, None], every_total, jnp.zeros((), jnp.float32)),
        axis=0,
    )
    return earlier[None]


def on_device(
    queries, keys, values, start_latent, out_weight, cfg_table, cfg_index, step_table, time_index
):
    step_dev, branches, heads, tok_dev, head_size = queries.shape
    groups = lax.axis_size("seq")
    steps_axis = lax.axis_size("step")
    items = step_dev * branches * heads
    per_dev = items // groups
    length = tok_dev * groups
    channels = out_weight.shape[0]
    me = lax.axis_index("seq")

    chunks = [a.reshape(groups, per_dev, tok_dev, head_size) for a in (queries, keys, values)]
    whole_steps = per_dev % (branches * heads) == 0
    if whole_steps and groups & (groups - 1) == 0:
        arrived = {}
        for k in reversed(range(groups)):
            pieces = [lax.dynamic_index_in_dim(c, me ^ k, 0, keepdims=False) for c in chunks]
            if k >= 2:
                sent = lax.ppermute(jnp.stack(pieces), "seq", xor_pairs(groups, k))
                pieces = [sent[i] for i in range(3)]
            elif k:
                pieces = [lax.ppermute(p, "seq", xor_pairs(groups, k)) for p in pieces]
            arrived[k] = pieces
        gathered = [
            jnp.concatenate([arrived[k][i] for k in range(groups)], axis=1) for i in range(3)
        ]
        partner_order = True
    else:
        stacked = jnp.stack(chunks, axis=1)
        gathered = lax.all_to_all(stacked, "seq", split_axis=0, concat_axis=3, tiled=True)
        gathered = gathered.reshape(3, per_dev, length, head_size)
        partner_order = False
    heads_out = attend(gathered[0], gathered[1], gathered[2])

    weight_heads = out_weight.reshape(channels, heads, head_size)
    guide_scale = lookup(cfg_table, cfg_index)[0]
    step_len = lookup(step_table, time_index)

    if whole_steps:
        local_steps = per_dev // (branches * heads)
        ho = heads_out.reshape(local_steps, branches, heads, length, head_size)
        wide = ho.astype(jnp.float32)
        square_sum = jnp.sum(wide * wide, axis=(2, 4))
        root_mean = jnp.sqrt(square_sum / (H * HD) + 1e-06)
        drift = (
            jnp.einsum("chd,sbhld->sblc", weight_heads, ho, preferred_element_type=jnp.float32)
            / root_mean[:, :, :, None]
        )
        my_len = lax.dynamic_slice_in_dim(step_len, me * local_steps, local_steps)
        shape = (local_steps, length, channels)
        scale_full, len_full, start_t = lax.optimization_barrier(
            (
                jnp.broadcast_to(guide_scale, shape),
                jnp.broadcast_to(my_len[:, None, None], shape),
                start_latent.T,
            )
        )
        guided = drift[:, 1] + scale_full * (drift[:, 0] - drift[:, 1])
        update = len_full * guided
        update = update.reshape(local_steps, groups, tok_dev, channels)
        return gather_prefix(
            update, start_t, me, groups, step_dev, steps_axis, partner_order
        )

    assert heads % per_dev == 0
    share = heads // per_dev
    first = me * per_dev
    head_ids = (first + jnp.arange(per_dev, dtype=jnp.int32)) % heads
    chosen = jnp.take(weight_heads, head_ids, axis=1)
    numer = jnp.einsum("cid,ild->cl", chosen, heads_out, preferred_element_type=jnp.float32)
    wide = heads_out.astype(jnp.float32)
    square = jnp.sum(wide * wide, axis=(0, 2))
    partial = jnp.concatenate([numer, square[None]], axis=0)
    partial = partial.reshape(channels + 1, groups, tok_dev)
    returned = lax.all_to_all(partial, "seq", split_axis=1, concat_axis=1, tiled=True)
    returned = returned.reshape(channels + 1, step_dev * branches, share, tok_dev)
    summed = jnp.sum(returned, axis=2).reshape(channels + 1, step_dev, branches, tok_dev)
    numer = jnp.transpose(summed[:channels], (1, 2, 0, 3))
    square_sum = summed[channels]
    root_mean = jnp.sqrt(square_sum / (H * HD) + 1e-06)
    drift = numer / root_mean[:, :, None, :]
    guided = drift[:, 1] + guide_scale * (drift[:, 0] - drift[:, 1])
    local_cum = jnp.cumsum(step_len[:, None, None] * guided, axis=0)
    return start_latent[None] + earlier_groups(local_cum, steps_axis) + local_cum


def solution(mesh):
    return jax.shard_map(
        on_device,
        mesh=mesh,
        in_specs=(
            P(("scene", "step"), None, None, "seq", None),
            P(("scene", "step"), None, None, "seq", None),
            P(("scene", "step"), None, None, "seq", None),
            P("scene", "seq"),
            P(),
            P(),
            P("scene"),
            P(),
            P(("scene", "step")),
        ),
        out_specs=P(("scene", "step"), None, "seq"),
        check_vma=False,
    )
```

```python
import jax
import jax.numpy as jnp
from jax import lax
from jax.sharding import PartitionSpec as P

HD = 128
H = 24


def lookup(table, index):
    count = table.shape[0]
    hits = index[..., None] == jnp.arange(count, dtype=jnp.int32)
    return jnp.sum(jnp.where(hits, table, jnp.zeros((), table.dtype)), axis=-1)


def attend(query_rows, key_rows, value_rows):
    scale = HD ** (-0.5)
    scores = (
        jnp.einsum("iqd,ikd->iqk", query_rows, key_rows, preferred_element_type=jnp.float32) * scale
    )
    expo = jnp.exp(scores - jnp.max(scores, axis=-1, keepdims=True))
    total = jnp.sum(expo, axis=-1, keepdims=True)
    weights = expo.astype(jnp.bfloat16)
    out = jnp.einsum("iqk,ikd->iqd", weights, value_rows, preferred_element_type=jnp.float32)
    return (out / total).astype(jnp.bfloat16)


def xor_pairs(size, k):
    return [(i, i ^ k) for i in range(size)]


def gather_prefix(update, start, me, groups, step_dev, steps_axis, partner_order):
    local_steps = update.shape[0]
    if partner_order:
        ordered = update
    else:
        partners = me ^ jnp.arange(groups, dtype=jnp.int32)
        ordered = jnp.take(update, partners, axis=1)
    pieces = [ordered[:, 0]]
    sources = [me]
    for k in range(1, groups):
        pieces.append(lax.ppermute(ordered[:, k], "seq", xor_pairs(groups, k)))
        sources.append(me ^ k)
    zero = jnp.zeros((), jnp.float32)
    outs = []
    for s in range(step_dev):
        acc = None
        for piece, source in zip(pieces, sources):
            for t in range(local_steps):
                term = jnp.where(source * local_steps + t <= s, piece[t], zero)
                acc = term if acc is None else acc + term
        outs.append(acc)
    total = outs[-1]
    local_cum = lax.optimization_barrier(jnp.stack(outs) + start[None])
    position = lax.axis_index("step")
    earlier = jnp.zeros_like(total)
    for k in range(1, steps_axis):
        other = lax.ppermute(total, "step", xor_pairs(steps_axis, k))
        earlier = earlier + jnp.where((position ^ k) < position, other, zero)
    return jnp.transpose(local_cum + earlier[None], (0, 2, 1))


def earlier_groups(local_cum, steps_axis):
    every_total = lax.all_gather(local_cum[-1][None], "step", axis=0, tiled=True)
    position = lax.axis_index("step")
    order = jnp.arange(steps_axis, dtype=jnp.int32)
    earlier = jnp.sum(
        jnp.where((order < position)[:, None, None], every_total, jnp.zeros((), jnp.float32)),
        axis=0,
    )
    return earlier[None]


def on_device(
    queries, keys, values, start_latent, out_weight, cfg_table, cfg_index, step_table, time_index
):
    step_dev, branches, heads, tok_dev, head_size = queries.shape
    groups = lax.axis_size("seq")
    steps_axis = lax.axis_size("step")
    items = step_dev * branches * heads
    per_dev = items // groups
    length = tok_dev * groups
    channels = out_weight.shape[0]
    me = lax.axis_index("seq")

    chunks = [a.reshape(groups, per_dev, tok_dev, head_size) for a in (queries, keys, values)]
    whole_steps = per_dev % (branches * heads) == 0
    if whole_steps and groups & (groups - 1) == 0:
        arrived = {}
        for k in reversed(range(groups)):
            pieces = [lax.dynamic_index_in_dim(c, me ^ k, 0, keepdims=False) for c in chunks]
            if k:
                pieces = [lax.ppermute(p, "seq", xor_pairs(groups, k)) for p in pieces]
            arrived[k] = pieces
        gathered = [
            jnp.concatenate([arrived[k][i] for k in range(groups)], axis=1) for i in range(3)
        ]
        partner_order = True
    else:
        stacked = jnp.stack(chunks, axis=1)
        gathered = lax.all_to_all(stacked, "seq", split_axis=0, concat_axis=3, tiled=True)
        gathered = gathered.reshape(3, per_dev, length, head_size)
        partner_order = False
    heads_out = attend(gathered[0], gathered[1], gathered[2])

    weight_heads = out_weight.reshape(channels, heads, head_size)
    guide_scale = lookup(cfg_table, cfg_index)[0]
    step_len = lookup(step_table, time_index)

    if whole_steps:
        local_steps = per_dev // (branches * heads)
        ho = heads_out.reshape(local_steps, branches, heads, length, head_size)
        wide = ho.astype(jnp.float32)
        square_sum = jnp.sum(wide * wide, axis=(2, 4))
        root_mean = jnp.sqrt(square_sum / (H * HD) + 1e-06)
        drift = (
            jnp.einsum("chd,sbhld->sblc", weight_heads, ho, preferred_element_type=jnp.float32)
            / root_mean[:, :, :, None]
        )
        owner = jnp.arange(step_dev, dtype=jnp.int32) // local_steps == me
        slot = jnp.arange(step_dev, dtype=jnp.int32) % local_steps
        mine = (owner[:, None] & (slot[:, None] == jnp.arange(local_steps)))[:, :, None, None]
        len_full = jnp.sum(
            jnp.where(mine, step_len[:, None, None, None], jnp.zeros((), jnp.float32)), axis=0
        )
        shape = (local_steps, length, channels)
        coef = lax.optimization_barrier(
            jnp.stack([jnp.broadcast_to(guide_scale, shape), jnp.broadcast_to(len_full, shape)])
        )
        scale_full, len_full = coef[0], coef[1]
        start_t = start_latent.T
        guided = drift[:, 1] + scale_full * (drift[:, 0] - drift[:, 1])
        update = len_full * guided
        update = update.reshape(local_steps, groups, tok_dev, channels)
        return gather_prefix(
            update, start_t, me, groups, step_dev, steps_axis, partner_order
        )

    assert heads % per_dev == 0
    share = heads // per_dev
    first = me * per_dev
    head_ids = (first + jnp.arange(per_dev, dtype=jnp.int32)) % heads
    chosen = jnp.take(weight_heads, head_ids, axis=1)
    numer = jnp.einsum("cid,ild->cl", chosen, heads_out, preferred_element_type=jnp.float32)
    wide = heads_out.astype(jnp.float32)
    square = jnp.sum(wide * wide, axis=(0, 2))
    partial = jnp.concatenate([numer, square[None]], axis=0)
    partial = partial.reshape(channels + 1, groups, tok_dev)
    returned = lax.all_to_all(partial, "seq", split_axis=1, concat_axis=1, tiled=True)
    returned = returned.reshape(channels + 1, step_dev * branches, share, tok_dev)
    summed = jnp.sum(returned, axis=2).reshape(channels + 1, step_dev, branches, tok_dev)
    numer = jnp.transpose(summed[:channels], (1, 2, 0, 3))
    square_sum = summed[channels]
    root_mean = jnp.sqrt(square_sum / (H * HD) + 1e-06)
    drift = numer / root_mean[:, :, None, :]
    guided = drift[:, 1] + guide_scale * (drift[:, 0] - drift[:, 1])
    local_cum = jnp.cumsum(step_len[:, None, None] * guided, axis=0)
    return start_latent[None] + earlier_groups(local_cum, steps_axis) + local_cum


def solution(mesh):
    return jax.shard_map(
        on_device,
        mesh=mesh,
        in_specs=(
            P(("scene", "step"), None, None, "seq", None),
            P(("scene", "step"), None, None, "seq", None),
            P(("scene", "step"), None, None, "seq", None),
            P("scene", "seq"),
            P(),
            P(),
            P("scene"),
            P(),
            P(("scene", "step")),
        ),
        out_specs=P(("scene", "step"), None, "seq"),
        check_vma=False,
    )
```

```python
import jax
import jax.numpy as jnp
from jax import lax
from jax.sharding import PartitionSpec as P

HD = 128
H = 24


def lookup(table, index):
    count = table.shape[0]
    hits = index[..., None] == jnp.arange(count, dtype=jnp.int32)
    return jnp.sum(jnp.where(hits, table, jnp.zeros((), table.dtype)), axis=-1)


def attend(query_rows, key_rows, value_rows):
    scale = HD ** (-0.5)
    scores = (
        jnp.einsum("iqd,ikd->iqk", query_rows, key_rows, preferred_element_type=jnp.float32) * scale
    )
    expo = jnp.exp(scores - jnp.max(scores, axis=-1, keepdims=True))
    total = jnp.sum(expo, axis=-1, keepdims=True)
    weights = expo.astype(jnp.bfloat16)
    out = jnp.einsum("iqk,ikd->iqd", weights, value_rows, preferred_element_type=jnp.float32)
    return (out / total).astype(jnp.bfloat16)


def xor_pairs(size, k):
    return [(i, i ^ k) for i in range(size)]


def gather_all_prefix(update, start, me, groups, step_dev, steps_axis, partner_order):
    local_steps = update.shape[0]
    if partner_order:
        natural = jnp.take(update, me ^ jnp.arange(groups, dtype=jnp.int32), axis=1)
    else:
        natural = update
    blocks = jnp.transpose(natural, (1, 0, 2, 3))
    sent = jnp.broadcast_to(blocks[None], (steps_axis,) + blocks.shape)
    sent = sent.reshape((steps_axis * groups,) + blocks.shape[1:])
    got = lax.all_to_all(sent, ("step", "seq"), split_axis=0, concat_axis=0, tiled=True)
    position = lax.axis_index("step")
    zero = jnp.zeros((), jnp.float32)
    outs = []
    for s in range(step_dev):
        acc = None
        for src in range(steps_axis * groups):
            for t in range(local_steps):
                step_of = (src // groups) * step_dev + (src % groups) * local_steps + t
                term = jnp.where(step_of <= position * step_dev + s, got[src, t], zero)
                acc = term if acc is None else acc + term
        outs.append(acc)
    local = jnp.stack(outs) + start[None]
    return jnp.transpose(local, (0, 2, 1))


def gather_prefix(update, start, me, groups, step_dev, steps_axis, partner_order):
    local_steps = update.shape[0]
    if partner_order:
        ordered = update
    else:
        partners = me ^ jnp.arange(groups, dtype=jnp.int32)
        ordered = jnp.take(update, partners, axis=1)
    pieces = [ordered[:, 0]]
    sources = [me]
    for k in range(1, groups):
        pieces.append(lax.ppermute(ordered[:, k], "seq", xor_pairs(groups, k)))
        sources.append(me ^ k)
    zero = jnp.zeros((), jnp.float32)
    outs = []
    for s in range(step_dev):
        acc = None
        for piece, source in zip(pieces, sources):
            for t in range(local_steps):
                term = jnp.where(source * local_steps + t <= s, piece[t], zero)
                acc = term if acc is None else acc + term
        outs.append(acc)
    total = outs[-1]
    local_cum = lax.optimization_barrier(jnp.stack(outs) + start[None])
    position = lax.axis_index("step")
    earlier = jnp.zeros_like(total)
    for k in range(1, steps_axis):
        other = lax.ppermute(total, "step", xor_pairs(steps_axis, k))
        earlier = earlier + jnp.where((position ^ k) < position, other, zero)
    return jnp.transpose(local_cum + earlier[None], (0, 2, 1))


def earlier_groups(local_cum, steps_axis):
    every_total = lax.all_gather(local_cum[-1][None], "step", axis=0, tiled=True)
    position = lax.axis_index("step")
    order = jnp.arange(steps_axis, dtype=jnp.int32)
    earlier = jnp.sum(
        jnp.where((order < position)[:, None, None], every_total, jnp.zeros((), jnp.float32)),
        axis=0,
    )
    return earlier[None]


def on_device(
    queries, keys, values, start_latent, out_weight, cfg_table, cfg_index, step_table, time_index
):
    step_dev, branches, heads, tok_dev, head_size = queries.shape
    groups = lax.axis_size("seq")
    steps_axis = lax.axis_size("step")
    items = step_dev * branches * heads
    per_dev = items // groups
    length = tok_dev * groups
    channels = out_weight.shape[0]
    me = lax.axis_index("seq")

    chunks = [a.reshape(groups, per_dev, tok_dev, head_size) for a in (queries, keys, values)]
    whole_steps = per_dev % (branches * heads) == 0
    if whole_steps and groups & (groups - 1) == 0:
        arrived = {}
        for k in reversed(range(groups)):
            pieces = [lax.dynamic_index_in_dim(c, me ^ k, 0, keepdims=False) for c in chunks]
            if k:
                pieces = [lax.ppermute(p, "seq", xor_pairs(groups, k)) for p in pieces]
            arrived[k] = pieces
        gathered = [
            jnp.concatenate([arrived[k][i] for k in range(groups)], axis=1) for i in range(3)
        ]
        partner_order = True
    else:
        stacked = jnp.stack(chunks, axis=1)
        gathered = lax.all_to_all(stacked, "seq", split_axis=0, concat_axis=3, tiled=True)
        gathered = gathered.reshape(3, per_dev, length, head_size)
        partner_order = False
    heads_out = attend(gathered[0], gathered[1], gathered[2])

    weight_heads = out_weight.reshape(channels, heads, head_size)
    guide_scale = lookup(cfg_table, cfg_index)[0]
    step_len = lookup(step_table, time_index)

    if whole_steps:
        local_steps = per_dev // (branches * heads)
        ho = heads_out.reshape(local_steps, branches, heads, length, head_size)
        wide = ho.astype(jnp.float32)
        square_sum = jnp.sum(wide * wide, axis=(2, 4))
        root_mean = jnp.sqrt(square_sum / (H * HD) + 1e-06)
        drift = (
            jnp.einsum("chd,sbhld->sblc", weight_heads, ho, preferred_element_type=jnp.float32)
            / root_mean[:, :, :, None]
        )
        owner = jnp.arange(step_dev, dtype=jnp.int32) // local_steps == me
        slot = jnp.arange(step_dev, dtype=jnp.int32) % local_steps
        mine = (owner[:, None] & (slot[:, None] == jnp.arange(local_steps)))[:, :, None, None]
        len_full = jnp.sum(
            jnp.where(mine, step_len[:, None, None, None], jnp.zeros((), jnp.float32)), axis=0
        )
        shape = (local_steps, length, channels)
        coef = lax.optimization_barrier(
            jnp.stack([jnp.broadcast_to(guide_scale, shape), jnp.broadcast_to(len_full, shape)])
        )
        scale_full, len_full = coef[0], coef[1]
        start_t = start_latent.T
        guided = drift[:, 1] + scale_full * (drift[:, 0] - drift[:, 1])
        update = len_full * guided
        update = update.reshape(local_steps, groups, tok_dev, channels)
        return gather_all_prefix(
            update, start_t, me, groups, step_dev, steps_axis, partner_order
        )

    assert heads % per_dev == 0
    share = heads // per_dev
    first = me * per_dev
    head_ids = (first + jnp.arange(per_dev, dtype=jnp.int32)) % heads
    chosen = jnp.take(weight_heads, head_ids, axis=1)
    numer = jnp.einsum("cid,ild->cl", chosen, heads_out, preferred_element_type=jnp.float32)
    wide = heads_out.astype(jnp.float32)
    square = jnp.sum(wide * wide, axis=(0, 2))
    partial = jnp.concatenate([numer, square[None]], axis=0)
    partial = partial.reshape(channels + 1, groups, tok_dev)
    returned = lax.all_to_all(partial, "seq", split_axis=1, concat_axis=1, tiled=True)
    returned = returned.reshape(channels + 1, step_dev * branches, share, tok_dev)
    summed = jnp.sum(returned, axis=2).reshape(channels + 1, step_dev, branches, tok_dev)
    numer = jnp.transpose(summed[:channels], (1, 2, 0, 3))
    square_sum = summed[channels]
    root_mean = jnp.sqrt(square_sum / (H * HD) + 1e-06)
    drift = numer / root_mean[:, :, None, :]
    guided = drift[:, 1] + guide_scale * (drift[:, 0] - drift[:, 1])
    local_cum = jnp.cumsum(step_len[:, None, None] * guided, axis=0)
    return start_latent[None] + earlier_groups(local_cum, steps_axis) + local_cum


def solution(mesh):
    return jax.shard_map(
        on_device,
        mesh=mesh,
        in_specs=(
            P(("scene", "step"), None, None, "seq", None),
            P(("scene", "step"), None, None, "seq", None),
            P(("scene", "step"), None, None, "seq", None),
            P("scene", "seq"),
            P(),
            P(),
            P("scene"),
            P(),
            P(("scene", "step")),
        ),
        out_specs=P(("scene", "step"), None, "seq"),
        check_vma=False,
    )
```

```python
import jax
import jax.numpy as jnp
from jax import lax
from jax.sharding import PartitionSpec as P

HD = 128
H = 24


def lookup(table, index):
    count = table.shape[0]
    hits = index[..., None] == jnp.arange(count, dtype=jnp.int32)
    return jnp.sum(jnp.where(hits, table, jnp.zeros((), table.dtype)), axis=-1)


def attend(query_rows, key_rows, value_rows):
    scale = HD ** (-0.5)
    scores = (
        jnp.einsum("iqd,ikd->iqk", query_rows, key_rows, preferred_element_type=jnp.float32) * scale
    )
    expo = jnp.exp(scores - jnp.max(scores, axis=-1, keepdims=True))
    total = jnp.sum(expo, axis=-1, keepdims=True)
    weights = expo.astype(jnp.bfloat16)
    out = jnp.einsum("iqk,ikd->iqd", weights, value_rows, preferred_element_type=jnp.float32)
    return (out / total).astype(jnp.bfloat16)


def xor_pairs(size, k):
    return [(i, i ^ k) for i in range(size)]


def gather_prefix(update, start, me, groups, step_dev, steps_axis, partner_order):
    local_steps = update.shape[0]
    if partner_order:
        ordered = update
    else:
        partners = me ^ jnp.arange(groups, dtype=jnp.int32)
        ordered = jnp.take(update, partners, axis=1)
    pieces = [ordered[:, 0]]
    sources = [me]
    for k in range(1, groups):
        pieces.append(lax.ppermute(ordered[:, k], "seq", xor_pairs(groups, k)))
        sources.append(me ^ k)
    zero = jnp.zeros((), jnp.float32)
    outs = []
    for s in range(step_dev):
        acc = None
        for piece, source in zip(pieces, sources):
            for t in range(local_steps):
                term = jnp.where(source * local_steps + t <= s, piece[t], zero)
                acc = term if acc is None else acc + term
        outs.append(acc)
    total = outs[-1]
    local_cum = lax.optimization_barrier(jnp.stack(outs) + start[None])
    position = lax.axis_index("step")
    earlier = jnp.zeros_like(total)
    for k in range(1, steps_axis):
        other = lax.ppermute(total, "step", xor_pairs(steps_axis, k))
        earlier = earlier + jnp.where((position ^ k) < position, other, zero)
    return jnp.transpose(local_cum + earlier[None], (0, 2, 1))


def earlier_groups(local_cum, steps_axis):
    every_total = lax.all_gather(local_cum[-1][None], "step", axis=0, tiled=True)
    position = lax.axis_index("step")
    order = jnp.arange(steps_axis, dtype=jnp.int32)
    earlier = jnp.sum(
        jnp.where((order < position)[:, None, None], every_total, jnp.zeros((), jnp.float32)),
        axis=0,
    )
    return earlier[None]


def on_device(
    queries, keys, values, start_latent, out_weight, cfg_table, cfg_index, step_table, time_index
):
    step_dev, branches, heads, tok_dev, head_size = queries.shape
    groups = lax.axis_size("seq")
    steps_axis = lax.axis_size("step")
    items = step_dev * branches * heads
    per_dev = items // groups
    length = tok_dev * groups
    channels = out_weight.shape[0]
    me = lax.axis_index("seq")

    chunks = [a.reshape(groups, per_dev, tok_dev, head_size) for a in (queries, keys, values)]
    whole_steps = per_dev % (branches * heads) == 0
    if whole_steps and groups & (groups - 1) == 0:
        arrived = {}
        for k in reversed(range(groups)):
            pieces = [lax.dynamic_index_in_dim(c, me ^ k, 0, keepdims=False) for c in chunks]
            if k:
                pieces = [lax.ppermute(p, "seq", xor_pairs(groups, k)) for p in pieces]
            arrived[k] = pieces
        gathered = [
            jnp.concatenate([arrived[k][i] for k in range(groups)], axis=1) for i in range(3)
        ]
        partner_order = True
    else:
        stacked = jnp.stack(chunks, axis=1)
        gathered = lax.all_to_all(stacked, "seq", split_axis=0, concat_axis=3, tiled=True)
        gathered = gathered.reshape(3, per_dev, length, head_size)
        partner_order = False
    if partner_order:
        far_q, cfg_table, cfg_index, step_table, time_index = lax.optimization_barrier(
            (arrived[groups - 1][0], cfg_table, cfg_index, step_table, time_index)
        )
        arrived[groups - 1][0] = far_q
        gathered[0] = jnp.concatenate([arrived[k][0] for k in range(groups)], axis=1)
    heads_out = attend(gathered[0], gathered[1], gathered[2])

    weight_heads = out_weight.reshape(channels, heads, head_size)
    guide_scale = lookup(cfg_table, cfg_index)[0]
    step_len = lookup(step_table, time_index)

    if whole_steps:
        local_steps = per_dev // (branches * heads)
        ho = heads_out.reshape(local_steps, branches, heads, length, head_size)
        wide = ho.astype(jnp.float32)
        square_sum = jnp.sum(wide * wide, axis=(2, 4))
        root_mean = jnp.sqrt(square_sum / (H * HD) + 1e-06)
        drift = (
            jnp.einsum("chd,sbhld->sblc", weight_heads, ho, preferred_element_type=jnp.float32)
            / root_mean[:, :, :, None]
        )
        owner = jnp.arange(step_dev, dtype=jnp.int32) // local_steps == me
        slot = jnp.arange(step_dev, dtype=jnp.int32) % local_steps
        mine = (owner[:, None] & (slot[:, None] == jnp.arange(local_steps)))[:, :, None, None]
        len_full = jnp.sum(
            jnp.where(mine, step_len[:, None, None, None], jnp.zeros((), jnp.float32)), axis=0
        )
        shape = (local_steps, length, channels)
        coef = lax.optimization_barrier(
            jnp.stack([jnp.broadcast_to(guide_scale, shape), jnp.broadcast_to(len_full, shape)])
        )
        scale_full, len_full = coef[0], coef[1]
        start_t = start_latent.T
        guided = drift[:, 1] + scale_full * (drift[:, 0] - drift[:, 1])
        update = len_full * guided
        update = update.reshape(local_steps, groups, tok_dev, channels)
        return gather_prefix(
            update, start_t, me, groups, step_dev, steps_axis, partner_order
        )

    assert heads % per_dev == 0
    share = heads // per_dev
    first = me * per_dev
    head_ids = (first + jnp.arange(per_dev, dtype=jnp.int32)) % heads
    chosen = jnp.take(weight_heads, head_ids, axis=1)
    numer = jnp.einsum("cid,ild->cl", chosen, heads_out, preferred_element_type=jnp.float32)
    wide = heads_out.astype(jnp.float32)
    square = jnp.sum(wide * wide, axis=(0, 2))
    partial = jnp.concatenate([numer, square[None]], axis=0)
    partial = partial.reshape(channels + 1, groups, tok_dev)
    returned = lax.all_to_all(partial, "seq", split_axis=1, concat_axis=1, tiled=True)
    returned = returned.reshape(channels + 1, step_dev * branches, share, tok_dev)
    summed = jnp.sum(returned, axis=2).reshape(channels + 1, step_dev, branches, tok_dev)
    numer = jnp.transpose(summed[:channels], (1, 2, 0, 3))
    square_sum = summed[channels]
    root_mean = jnp.sqrt(square_sum / (H * HD) + 1e-06)
    drift = numer / root_mean[:, :, None, :]
    guided = drift[:, 1] + guide_scale * (drift[:, 0] - drift[:, 1])
    local_cum = jnp.cumsum(step_len[:, None, None] * guided, axis=0)
    return start_latent[None] + earlier_groups(local_cum, steps_axis) + local_cum


def solution(mesh):
    return jax.shard_map(
        on_device,
        mesh=mesh,
        in_specs=(
            P(("scene", "step"), None, None, "seq", None),
            P(("scene", "step"), None, None, "seq", None),
            P(("scene", "step"), None, None, "seq", None),
            P("scene", "seq"),
            P(),
            P(),
            P("scene"),
            P(),
            P(("scene", "step")),
        ),
        out_specs=P(("scene", "step"), None, "seq"),
        check_vma=False,
    )
```

```python
import jax
import jax.numpy as jnp
from jax import lax
from jax.sharding import PartitionSpec as P

HD = 128
H = 24


def lookup(table, index):
    count = table.shape[0]
    hits = index[..., None] == jnp.arange(count, dtype=jnp.int32)
    return jnp.sum(jnp.where(hits, table, jnp.zeros((), table.dtype)), axis=-1)


def attend(query_rows, key_rows, value_rows):
    scale = HD ** (-0.5)
    scores = (
        jnp.einsum("iqd,ikd->iqk", query_rows, key_rows, preferred_element_type=jnp.float32) * scale
    )
    expo = jnp.exp(scores - jnp.max(scores, axis=-1, keepdims=True))
    total = jnp.sum(expo, axis=-1, keepdims=True)
    weights = expo.astype(jnp.bfloat16)
    out = jnp.einsum("iqk,ikd->iqd", weights, value_rows, preferred_element_type=jnp.float32)
    return (out / total).astype(jnp.bfloat16)


def xor_pairs(size, k):
    return [(i, i ^ k) for i in range(size)]


def gather_prefix(update, start, me, groups, step_dev, steps_axis, partner_order):
    local_steps = update.shape[0]
    if partner_order:
        ordered = update
    else:
        partners = me ^ jnp.arange(groups, dtype=jnp.int32)
        ordered = jnp.take(update, partners, axis=1)
    pieces = [ordered[:, 0]]
    sources = [me]
    for k in range(1, groups):
        pieces.append(lax.ppermute(ordered[:, k], "seq", xor_pairs(groups, k)))
        sources.append(me ^ k)
    zero = jnp.zeros((), jnp.float32)
    outs = []
    for s in range(step_dev):
        acc = None
        for piece, source in zip(pieces, sources):
            for t in range(local_steps):
                term = jnp.where(source * local_steps + t <= s, piece[t], zero)
                acc = term if acc is None else acc + term
        outs.append(acc)
    total = outs[-1]
    local_cum = lax.optimization_barrier(jnp.stack(outs) + start[None])
    position = lax.axis_index("step")
    earlier = jnp.zeros_like(total)
    for k in range(1, steps_axis):
        other = lax.ppermute(total, "step", xor_pairs(steps_axis, k))
        earlier = earlier + jnp.where((position ^ k) < position, other, zero)
    return jnp.transpose(local_cum + earlier[None], (0, 2, 1))


def earlier_groups(local_cum, steps_axis):
    every_total = lax.all_gather(local_cum[-1][None], "step", axis=0, tiled=True)
    position = lax.axis_index("step")
    order = jnp.arange(steps_axis, dtype=jnp.int32)
    earlier = jnp.sum(
        jnp.where((order < position)[:, None, None], every_total, jnp.zeros((), jnp.float32)),
        axis=0,
    )
    return earlier[None]


def on_device(
    queries, keys, values, start_latent, out_weight, cfg_table, cfg_index, step_table, time_index
):
    step_dev, branches, heads, tok_dev, head_size = queries.shape
    groups = lax.axis_size("seq")
    steps_axis = lax.axis_size("step")
    items = step_dev * branches * heads
    per_dev = items // groups
    length = tok_dev * groups
    channels = out_weight.shape[0]
    me = lax.axis_index("seq")

    chunks = [a.reshape(groups, per_dev, tok_dev, head_size) for a in (queries, keys, values)]
    whole_steps = per_dev % (branches * heads) == 0
    if whole_steps and groups & (groups - 1) == 0:
        arrived = {}
        for k in reversed(range(groups)):
            pieces = [lax.dynamic_index_in_dim(c, me ^ k, 0, keepdims=False) for c in chunks]
            if k:
                pieces = [lax.ppermute(p, "seq", xor_pairs(groups, k)) for p in pieces]
            arrived[k] = pieces
        gathered = [
            jnp.concatenate([arrived[k][i] for k in range(groups)], axis=1) for i in range(3)
        ]
        partner_order = True
    else:
        stacked = jnp.stack(chunks, axis=1)
        gathered = lax.all_to_all(stacked, "seq", split_axis=0, concat_axis=3, tiled=True)
        gathered = gathered.reshape(3, per_dev, length, head_size)
        partner_order = False
    if partner_order:
        near_q, cfg_table, cfg_index, step_table, time_index = lax.optimization_barrier(
            (arrived[1][0], cfg_table, cfg_index, step_table, time_index)
        )
        arrived[1][0] = near_q
        gathered[0] = jnp.concatenate([arrived[k][0] for k in range(groups)], axis=1)

    weight_heads = out_weight.reshape(channels, heads, head_size)
    guide_scale = lookup(cfg_table, cfg_index)[0]
    step_len = lookup(step_table, time_index)

    if whole_steps:
        local_steps = per_dev // (branches * heads)
        owner = jnp.arange(step_dev, dtype=jnp.int32) // local_steps == me
        slot = jnp.arange(step_dev, dtype=jnp.int32) % local_steps
        mine = (owner[:, None] & (slot[:, None] == jnp.arange(local_steps)))[:, :, None, None]
        len_full = jnp.sum(
            jnp.where(mine, step_len[:, None, None, None], jnp.zeros((), jnp.float32)), axis=0
        )
        shape = (local_steps, length, channels)
        coef = jnp.stack([jnp.broadcast_to(guide_scale, shape), jnp.broadcast_to(len_full, shape)])
        gathered[0], coef = lax.optimization_barrier((gathered[0], coef))
    heads_out = attend(gathered[0], gathered[1], gathered[2])

    if whole_steps:
        ho = heads_out.reshape(local_steps, branches, heads, length, head_size)
        wide = ho.astype(jnp.float32)
        square_sum = jnp.sum(wide * wide, axis=(2, 4))
        root_mean = jnp.sqrt(square_sum / (H * HD) + 1e-06)
        drift = (
            jnp.einsum("chd,sbhld->sblc", weight_heads, ho, preferred_element_type=jnp.float32)
            / root_mean[:, :, :, None]
        )
        scale_full, len_full = coef[0], coef[1]
        start_t = start_latent.T
        guided = drift[:, 1] + scale_full * (drift[:, 0] - drift[:, 1])
        update = len_full * guided
        update = update.reshape(local_steps, groups, tok_dev, channels)
        return gather_prefix(
            update, start_t, me, groups, step_dev, steps_axis, partner_order
        )

    assert heads % per_dev == 0
    share = heads // per_dev
    first = me * per_dev
    head_ids = (first + jnp.arange(per_dev, dtype=jnp.int32)) % heads
    chosen = jnp.take(weight_heads, head_ids, axis=1)
    numer = jnp.einsum("cid,ild->cl", chosen, heads_out, preferred_element_type=jnp.float32)
    wide = heads_out.astype(jnp.float32)
    square = jnp.sum(wide * wide, axis=(0, 2))
    partial = jnp.concatenate([numer, square[None]], axis=0)
    partial = partial.reshape(channels + 1, groups, tok_dev)
    returned = lax.all_to_all(partial, "seq", split_axis=1, concat_axis=1, tiled=True)
    returned = returned.reshape(channels + 1, step_dev * branches, share, tok_dev)
    summed = jnp.sum(returned, axis=2).reshape(channels + 1, step_dev, branches, tok_dev)
    numer = jnp.transpose(summed[:channels], (1, 2, 0, 3))
    square_sum = summed[channels]
    root_mean = jnp.sqrt(square_sum / (H * HD) + 1e-06)
    drift = numer / root_mean[:, :, None, :]
    guided = drift[:, 1] + guide_scale * (drift[:, 0] - drift[:, 1])
    local_cum = jnp.cumsum(step_len[:, None, None] * guided, axis=0)
    return start_latent[None] + earlier_groups(local_cum, steps_axis) + local_cum


def solution(mesh):
    return jax.shard_map(
        on_device,
        mesh=mesh,
        in_specs=(
            P(("scene", "step"), None, None, "seq", None),
            P(("scene", "step"), None, None, "seq", None),
            P(("scene", "step"), None, None, "seq", None),
            P("scene", "seq"),
            P(),
            P(),
            P("scene"),
            P(),
            P(("scene", "step")),
        ),
        out_specs=P(("scene", "step"), None, "seq"),
        check_vma=False,
    )
```

```python
import jax
import jax.numpy as jnp
from jax import lax
from jax.sharding import PartitionSpec as P

HD = 128
H = 24


def lookup(table, index):
    count = table.shape[0]
    hits = index[..., None] == jnp.arange(count, dtype=jnp.int32)
    return jnp.sum(jnp.where(hits, table, jnp.zeros((), table.dtype)), axis=-1)


def attend(query_rows, key_rows, value_rows):
    scale = HD ** (-0.5)
    scores = (
        jnp.einsum("iqd,ikd->iqk", query_rows, key_rows, preferred_element_type=jnp.float32) * scale
    )
    expo = jnp.exp(scores - jnp.max(scores, axis=-1, keepdims=True))
    total = jnp.sum(expo, axis=-1, keepdims=True)
    weights = expo.astype(jnp.bfloat16)
    if isinstance(value_rows, list):
        out = None
        first = 0
        for block in value_rows:
            size = block.shape[1]
            part = jnp.einsum(
                "iqk,ikd->iqd",
                weights[:, :, first : first + size],
                block,
                preferred_element_type=jnp.float32,
            )
            out = part if out is None else out + part
            first += size
    else:
        out = jnp.einsum("iqk,ikd->iqd", weights, value_rows, preferred_element_type=jnp.float32)
    return (out / total).astype(jnp.bfloat16)


def xor_pairs(size, k):
    return [(i, i ^ k) for i in range(size)]


def gather_prefix(update, start, me, groups, step_dev, steps_axis, partner_order):
    local_steps = update.shape[0]
    if partner_order:
        ordered = update
    else:
        partners = me ^ jnp.arange(groups, dtype=jnp.int32)
        ordered = jnp.take(update, partners, axis=1)
    pieces = [ordered[:, 0]]
    sources = [me]
    for k in range(1, groups):
        pieces.append(lax.ppermute(ordered[:, k], "seq", xor_pairs(groups, k)))
        sources.append(me ^ k)
    zero = jnp.zeros((), jnp.float32)
    outs = []
    for s in range(step_dev):
        acc = None
        for piece, source in zip(pieces, sources):
            for t in range(local_steps):
                term = jnp.where(source * local_steps + t <= s, piece[t], zero)
                acc = term if acc is None else acc + term
        outs.append(acc)
    total = outs[-1]
    local_cum = lax.optimization_barrier(jnp.stack(outs) + start[None])
    position = lax.axis_index("step")
    earlier = jnp.zeros_like(total)
    for k in range(1, steps_axis):
        other = lax.ppermute(total, "step", xor_pairs(steps_axis, k))
        earlier = earlier + jnp.where((position ^ k) < position, other, zero)
    return jnp.transpose(local_cum + earlier[None], (0, 2, 1))


def earlier_groups(local_cum, steps_axis):
    every_total = lax.all_gather(local_cum[-1][None], "step", axis=0, tiled=True)
    position = lax.axis_index("step")
    order = jnp.arange(steps_axis, dtype=jnp.int32)
    earlier = jnp.sum(
        jnp.where((order < position)[:, None, None], every_total, jnp.zeros((), jnp.float32)),
        axis=0,
    )
    return earlier[None]


def on_device(
    queries, keys, values, start_latent, out_weight, cfg_table, cfg_index, step_table, time_index
):
    step_dev, branches, heads, tok_dev, head_size = queries.shape
    groups = lax.axis_size("seq")
    steps_axis = lax.axis_size("step")
    items = step_dev * branches * heads
    per_dev = items // groups
    length = tok_dev * groups
    channels = out_weight.shape[0]
    me = lax.axis_index("seq")

    chunks = [a.reshape(groups, per_dev, tok_dev, head_size) for a in (queries, keys, values)]
    whole_steps = per_dev % (branches * heads) == 0
    if whole_steps and groups & (groups - 1) == 0:
        arrived = {}
        for k in reversed(range(groups)):
            pieces = [lax.dynamic_index_in_dim(c, me ^ k, 0, keepdims=False) for c in chunks]
            if k:
                pieces = [lax.ppermute(p, "seq", xor_pairs(groups, k)) for p in pieces]
            arrived[k] = pieces
        gathered = [
            jnp.concatenate([arrived[k][i] for k in range(groups)], axis=1) for i in range(2)
        ]
        gathered.append([arrived[k][2] for k in range(groups)])
        partner_order = True
    else:
        stacked = jnp.stack(chunks, axis=1)
        gathered = lax.all_to_all(stacked, "seq", split_axis=0, concat_axis=3, tiled=True)
        gathered = gathered.reshape(3, per_dev, length, head_size)
        partner_order = False
    heads_out = attend(gathered[0], gathered[1], gathered[2])

    weight_heads = out_weight.reshape(channels, heads, head_size)
    guide_scale = lookup(cfg_table, cfg_index)[0]
    step_len = lookup(step_table, time_index)

    if whole_steps:
        local_steps = per_dev // (branches * heads)
        ho = heads_out.reshape(local_steps, branches, heads, length, head_size)
        wide = ho.astype(jnp.float32)
        square_sum = jnp.sum(wide * wide, axis=(2, 4))
        root_mean = jnp.sqrt(square_sum / (H * HD) + 1e-06)
        drift = (
            jnp.einsum("chd,sbhld->sblc", weight_heads, ho, preferred_element_type=jnp.float32)
            / root_mean[:, :, :, None]
        )
        owner = jnp.arange(step_dev, dtype=jnp.int32) // local_steps == me
        slot = jnp.arange(step_dev, dtype=jnp.int32) % local_steps
        mine = (owner[:, None] & (slot[:, None] == jnp.arange(local_steps)))[:, :, None, None]
        len_full = jnp.sum(
            jnp.where(mine, step_len[:, None, None, None], jnp.zeros((), jnp.float32)), axis=0
        )
        shape = (local_steps, length, channels)
        coef = lax.optimization_barrier(
            jnp.stack([jnp.broadcast_to(guide_scale, shape), jnp.broadcast_to(len_full, shape)])
        )
        scale_full, len_full = coef[0], coef[1]
        start_t = start_latent.T
        guided = drift[:, 1] + scale_full * (drift[:, 0] - drift[:, 1])
        update = len_full * guided
        update = update.reshape(local_steps, groups, tok_dev, channels)
        return gather_prefix(
            update, start_t, me, groups, step_dev, steps_axis, partner_order
        )

    assert heads % per_dev == 0
    share = heads // per_dev
    first = me * per_dev
    head_ids = (first + jnp.arange(per_dev, dtype=jnp.int32)) % heads
    chosen = jnp.take(weight_heads, head_ids, axis=1)
    numer = jnp.einsum("cid,ild->cl", chosen, heads_out, preferred_element_type=jnp.float32)
    wide = heads_out.astype(jnp.float32)
    square = jnp.sum(wide * wide, axis=(0, 2))
    partial = jnp.concatenate([numer, square[None]], axis=0)
    partial = partial.reshape(channels + 1, groups, tok_dev)
    returned = lax.all_to_all(partial, "seq", split_axis=1, concat_axis=1, tiled=True)
    returned = returned.reshape(channels + 1, step_dev * branches, share, tok_dev)
    summed = jnp.sum(returned, axis=2).reshape(channels + 1, step_dev, branches, tok_dev)
    numer = jnp.transpose(summed[:channels], (1, 2, 0, 3))
    square_sum = summed[channels]
    root_mean = jnp.sqrt(square_sum / (H * HD) + 1e-06)
    drift = numer / root_mean[:, :, None, :]
    guided = drift[:, 1] + guide_scale * (drift[:, 0] - drift[:, 1])
    local_cum = jnp.cumsum(step_len[:, None, None] * guided, axis=0)
    return start_latent[None] + earlier_groups(local_cum, steps_axis) + local_cum


def solution(mesh):
    return jax.shard_map(
        on_device,
        mesh=mesh,
        in_specs=(
            P(("scene", "step"), None, None, "seq", None),
            P(("scene", "step"), None, None, "seq", None),
            P(("scene", "step"), None, None, "seq", None),
            P("scene", "seq"),
            P(),
            P(),
            P("scene"),
            P(),
            P(("scene", "step")),
        ),
        out_specs=P(("scene", "step"), None, "seq"),
        check_vma=False,
    )
```

```python
import jax
import jax.numpy as jnp
from jax import lax
from jax.sharding import PartitionSpec as P

HD = 128
H = 24


def lookup(table, index):
    count = table.shape[0]
    hits = index[..., None] == jnp.arange(count, dtype=jnp.int32)
    return jnp.sum(jnp.where(hits, table, jnp.zeros((), table.dtype)), axis=-1)


def attend(query_rows, key_rows, value_rows):
    scale = HD ** (-0.5)
    scores = (
        jnp.einsum("iqd,ikd->iqk", query_rows, key_rows, preferred_element_type=jnp.float32) * scale
    )
    expo = jnp.exp(scores - jnp.max(scores, axis=-1, keepdims=True))
    total = jnp.sum(expo, axis=-1, keepdims=True)
    weights = expo.astype(jnp.bfloat16)
    if isinstance(value_rows, list):
        out = None
        first = 0
        for block in value_rows:
            size = block.shape[1]
            part = jnp.einsum(
                "iqk,ikd->iqd",
                weights[:, :, first : first + size],
                block,
                preferred_element_type=jnp.float32,
            )
            out = part if out is None else out + part
            first += size
    else:
        out = jnp.einsum("iqk,ikd->iqd", weights, value_rows, preferred_element_type=jnp.float32)
    return (out / total).astype(jnp.bfloat16)


def xor_pairs(size, k):
    return [(i, i ^ k) for i in range(size)]


def prefix_from_pieces(pieces, sources, start, step_dev, steps_axis):
    local_steps = pieces[0].shape[0]
    zero = jnp.zeros((), jnp.float32)
    outs = []
    for s in range(step_dev):
        acc = None
        for piece, source in zip(pieces, sources):
            for t in range(local_steps):
                term = jnp.where(source * local_steps + t <= s, piece[t], zero)
                acc = term if acc is None else acc + term
        outs.append(acc)
    total = outs[-1]
    local_cum = lax.optimization_barrier(jnp.stack(outs) + start[None])
    position = lax.axis_index("step")
    earlier = jnp.zeros_like(total)
    for k in range(1, steps_axis):
        other = lax.ppermute(total, "step", xor_pairs(steps_axis, k))
        earlier = earlier + jnp.where((position ^ k) < position, other, zero)
    return jnp.transpose(local_cum + earlier[None], (0, 2, 1))


def gather_prefix(update, start, me, groups, step_dev, steps_axis, partner_order):
    local_steps = update.shape[0]
    if partner_order:
        ordered = update
    else:
        partners = me ^ jnp.arange(groups, dtype=jnp.int32)
        ordered = jnp.take(update, partners, axis=1)
    pieces = [ordered[:, 0]]
    sources = [me]
    for k in range(1, groups):
        pieces.append(lax.ppermute(ordered[:, k], "seq", xor_pairs(groups, k)))
        sources.append(me ^ k)
    zero = jnp.zeros((), jnp.float32)
    outs = []
    for s in range(step_dev):
        acc = None
        for piece, source in zip(pieces, sources):
            for t in range(local_steps):
                term = jnp.where(source * local_steps + t <= s, piece[t], zero)
                acc = term if acc is None else acc + term
        outs.append(acc)
    total = outs[-1]
    local_cum = lax.optimization_barrier(jnp.stack(outs) + start[None])
    position = lax.axis_index("step")
    earlier = jnp.zeros_like(total)
    for k in range(1, steps_axis):
        other = lax.ppermute(total, "step", xor_pairs(steps_axis, k))
        earlier = earlier + jnp.where((position ^ k) < position, other, zero)
    return jnp.transpose(local_cum + earlier[None], (0, 2, 1))


def earlier_groups(local_cum, steps_axis):
    every_total = lax.all_gather(local_cum[-1][None], "step", axis=0, tiled=True)
    position = lax.axis_index("step")
    order = jnp.arange(steps_axis, dtype=jnp.int32)
    earlier = jnp.sum(
        jnp.where((order < position)[:, None, None], every_total, jnp.zeros((), jnp.float32)),
        axis=0,
    )
    return earlier[None]


def on_device(
    queries, keys, values, start_latent, out_weight, cfg_table, cfg_index, step_table, time_index
):
    step_dev, branches, heads, tok_dev, head_size = queries.shape
    groups = lax.axis_size("seq")
    steps_axis = lax.axis_size("step")
    items = step_dev * branches * heads
    per_dev = items // groups
    length = tok_dev * groups
    channels = out_weight.shape[0]
    me = lax.axis_index("seq")

    chunks = [a.reshape(groups, per_dev, tok_dev, head_size) for a in (queries, keys, values)]
    whole_steps = per_dev % (branches * heads) == 0
    partner_order = whole_steps and groups & (groups - 1) == 0
    if partner_order:
        arrived = {}
        for k in reversed(range(groups)):
            sent = [lax.dynamic_index_in_dim(c, me ^ k, 0, keepdims=False) for c in chunks[::-1]]
            if k:
                sent = [lax.ppermute(p, "seq", xor_pairs(groups, k)) for p in sent]
            arrived[k] = sent[::-1]
    else:
        stacked = jnp.stack(chunks, axis=1)
        gathered = lax.all_to_all(stacked, "seq", split_axis=0, concat_axis=3, tiled=True)
        gathered = gathered.reshape(3, per_dev, length, head_size)

    weight_heads = out_weight.reshape(channels, heads, head_size)
    guide_scale = lookup(cfg_table, cfg_index)[0]
    step_len = lookup(step_table, time_index)

    if whole_steps:
        local_steps = per_dev // (branches * heads)
        rows = tok_dev if partner_order else length
        owner = jnp.arange(step_dev, dtype=jnp.int32) // local_steps == me
        slot = jnp.arange(step_dev, dtype=jnp.int32) % local_steps
        mine = (owner[:, None] & (slot[:, None] == jnp.arange(local_steps)))[:, :, None, None]
        len_full = jnp.sum(
            jnp.where(mine, step_len[:, None, None, None], jnp.zeros((), jnp.float32)), axis=0
        )
        shape = (local_steps, rows, channels)
        coef = lax.optimization_barrier(
            jnp.stack([jnp.broadcast_to(guide_scale, shape), jnp.broadcast_to(len_full, shape)])
        )
        scale_full, len_full = coef[0], coef[1]
        start_t = start_latent.T

        def finish(heads_out):
            ho = heads_out.reshape(local_steps, branches, heads, rows, head_size)
            wide = ho.astype(jnp.float32)
            square_sum = jnp.sum(wide * wide, axis=(2, 4))
            root_mean = jnp.sqrt(square_sum / (H * HD) + 1e-06)
            drift = (
                jnp.einsum("chd,sbhld->sblc", weight_heads, ho, preferred_element_type=jnp.float32)
                / root_mean[:, :, :, None]
            )
            guided = drift[:, 1] + scale_full * (drift[:, 0] - drift[:, 1])
            return len_full * guided

        if partner_order:
            keys_all = jnp.concatenate([arrived[k][1] for k in range(groups)], axis=1)
            values_list = [arrived[k][2] for k in range(groups)]
            pieces = []
            for k in range(groups):
                piece = finish(attend(arrived[k][0], keys_all, values_list))
                if k:
                    piece = lax.ppermute(piece, "seq", xor_pairs(groups, k))
                pieces.append(piece)
            sources = [me ^ k for k in range(groups)]
            return prefix_from_pieces(pieces, sources, start_t, step_dev, steps_axis)
        update = finish(attend(gathered[0], gathered[1], gathered[2]))
        update = update.reshape(local_steps, groups, tok_dev, channels)
        return gather_prefix(update, start_t, me, groups, step_dev, steps_axis, False)

    heads_out = attend(gathered[0], gathered[1], gathered[2])

    assert heads % per_dev == 0
    share = heads // per_dev
    first = me * per_dev
    head_ids = (first + jnp.arange(per_dev, dtype=jnp.int32)) % heads
    chosen = jnp.take(weight_heads, head_ids, axis=1)
    numer = jnp.einsum("cid,ild->cl", chosen, heads_out, preferred_element_type=jnp.float32)
    wide = heads_out.astype(jnp.float32)
    square = jnp.sum(wide * wide, axis=(0, 2))
    partial = jnp.concatenate([numer, square[None]], axis=0)
    partial = partial.reshape(channels + 1, groups, tok_dev)
    returned = lax.all_to_all(partial, "seq", split_axis=1, concat_axis=1, tiled=True)
    returned = returned.reshape(channels + 1, step_dev * branches, share, tok_dev)
    summed = jnp.sum(returned, axis=2).reshape(channels + 1, step_dev, branches, tok_dev)
    numer = jnp.transpose(summed[:channels], (1, 2, 0, 3))
    square_sum = summed[channels]
    root_mean = jnp.sqrt(square_sum / (H * HD) + 1e-06)
    drift = numer / root_mean[:, :, None, :]
    guided = drift[:, 1] + guide_scale * (drift[:, 0] - drift[:, 1])
    local_cum = jnp.cumsum(step_len[:, None, None] * guided, axis=0)
    return start_latent[None] + earlier_groups(local_cum, steps_axis) + local_cum


def solution(mesh):
    return jax.shard_map(
        on_device,
        mesh=mesh,
        in_specs=(
            P(("scene", "step"), None, None, "seq", None),
            P(("scene", "step"), None, None, "seq", None),
            P(("scene", "step"), None, None, "seq", None),
            P("scene", "seq"),
            P(),
            P(),
            P("scene"),
            P(),
            P(("scene", "step")),
        ),
        out_specs=P(("scene", "step"), None, "seq"),
        check_vma=False,
    )
```

```python
import jax
import jax.numpy as jnp
from jax import lax
from jax.sharding import PartitionSpec as P

HD = 128
H = 24


def lookup(table, index):
    count = table.shape[0]
    hits = index[..., None] == jnp.arange(count, dtype=jnp.int32)
    return jnp.sum(jnp.where(hits, table, jnp.zeros((), table.dtype)), axis=-1)


def attend(query_rows, key_rows, value_rows):
    scale = HD ** (-0.5)
    scores = (
        jnp.einsum("iqd,ikd->iqk", query_rows, key_rows, preferred_element_type=jnp.float32) * scale
    )
    expo = jnp.exp(scores - jnp.max(scores, axis=-1, keepdims=True))
    total = jnp.sum(expo, axis=-1, keepdims=True)
    weights = expo.astype(jnp.bfloat16)
    if isinstance(value_rows, list):
        out = None
        first = 0
        for block in value_rows:
            size = block.shape[1]
            part = jnp.einsum(
                "iqk,ikd->iqd",
                weights[:, :, first : first + size],
                block,
                preferred_element_type=jnp.float32,
            )
            out = part if out is None else out + part
            first += size
    else:
        out = jnp.einsum("iqk,ikd->iqd", weights, value_rows, preferred_element_type=jnp.float32)
    return (out / total).astype(jnp.bfloat16)


def xor_pairs(size, k):
    return [(i, i ^ k) for i in range(size)]


def gather_prefix(update, start, me, groups, step_dev, steps_axis, partner_order):
    local_steps = update.shape[0]
    if partner_order:
        ordered = update
    else:
        partners = me ^ jnp.arange(groups, dtype=jnp.int32)
        ordered = jnp.take(update, partners, axis=1)
    every = lax.all_gather(ordered, "seq", axis=0, tiled=False)
    pieces = []
    sources = []
    for j in range(groups):
        pieces.append(lax.dynamic_index_in_dim(every[j], j ^ me, 1, keepdims=False))
        sources.append(j)
    zero = jnp.zeros((), jnp.float32)
    outs = []
    for s in range(step_dev):
        acc = None
        for piece, source in zip(pieces, sources):
            for t in range(local_steps):
                term = jnp.where(source * local_steps + t <= s, piece[t], zero)
                acc = term if acc is None else acc + term
        outs.append(acc)
    total = outs[-1]
    local_cum = lax.optimization_barrier(jnp.stack(outs) + start[None])
    position = lax.axis_index("step")
    earlier = jnp.zeros_like(total)
    for k in range(1, steps_axis):
        other = lax.ppermute(total, "step", xor_pairs(steps_axis, k))
        earlier = earlier + jnp.where((position ^ k) < position, other, zero)
    return jnp.transpose(local_cum + earlier[None], (0, 2, 1))


def earlier_groups(local_cum, steps_axis):
    every_total = lax.all_gather(local_cum[-1][None], "step", axis=0, tiled=True)
    position = lax.axis_index("step")
    order = jnp.arange(steps_axis, dtype=jnp.int32)
    earlier = jnp.sum(
        jnp.where((order < position)[:, None, None], every_total, jnp.zeros((), jnp.float32)),
        axis=0,
    )
    return earlier[None]


def on_device(
    queries, keys, values, start_latent, out_weight, cfg_table, cfg_index, step_table, time_index
):
    step_dev, branches, heads, tok_dev, head_size = queries.shape
    groups = lax.axis_size("seq")
    steps_axis = lax.axis_size("step")
    items = step_dev * branches * heads
    per_dev = items // groups
    length = tok_dev * groups
    channels = out_weight.shape[0]
    me = lax.axis_index("seq")

    chunks = [a.reshape(groups, per_dev, tok_dev, head_size) for a in (queries, keys, values)]
    whole_steps = per_dev % (branches * heads) == 0
    if whole_steps and groups & (groups - 1) == 0:
        arrived = {}
        for k in reversed(range(groups)):
            pieces = [lax.dynamic_index_in_dim(c, me ^ k, 0, keepdims=False) for c in chunks]
            if k:
                pieces = [lax.ppermute(p, "seq", xor_pairs(groups, k)) for p in pieces]
            arrived[k] = pieces
        gathered = [
            jnp.concatenate([arrived[k][i] for k in range(groups)], axis=1) for i in range(2)
        ]
        gathered.append([arrived[k][2] for k in range(groups)])
        partner_order = True
    else:
        stacked = jnp.stack(chunks, axis=1)
        gathered = lax.all_to_all(stacked, "seq", split_axis=0, concat_axis=3, tiled=True)
        gathered = gathered.reshape(3, per_dev, length, head_size)
        partner_order = False
    heads_out = attend(gathered[0], gathered[1], gathered[2])

    weight_heads = out_weight.reshape(channels, heads, head_size)
    guide_scale = lookup(cfg_table, cfg_index)[0]
    step_len = lookup(step_table, time_index)

    if whole_steps:
        local_steps = per_dev // (branches * heads)
        ho = heads_out.reshape(local_steps, branches, heads, length, head_size)
        wide = ho.astype(jnp.float32)
        square_sum = jnp.sum(wide * wide, axis=(2, 4))
        root_mean = jnp.sqrt(square_sum / (H * HD) + 1e-06)
        drift = (
            jnp.einsum("chd,sbhld->sblc", weight_heads, ho, preferred_element_type=jnp.float32)
            / root_mean[:, :, :, None]
        )
        owner = jnp.arange(step_dev, dtype=jnp.int32) // local_steps == me
        slot = jnp.arange(step_dev, dtype=jnp.int32) % local_steps
        mine = (owner[:, None] & (slot[:, None] == jnp.arange(local_steps)))[:, :, None, None]
        len_full = jnp.sum(
            jnp.where(mine, step_len[:, None, None, None], jnp.zeros((), jnp.float32)), axis=0
        )
        shape = (local_steps, length, channels)
        coef = lax.optimization_barrier(
            jnp.stack([jnp.broadcast_to(guide_scale, shape), jnp.broadcast_to(len_full, shape)])
        )
        scale_full, len_full = coef[0], coef[1]
        start_t = start_latent.T
        guided = drift[:, 1] + scale_full * (drift[:, 0] - drift[:, 1])
        update = len_full * guided
        update = update.reshape(local_steps, groups, tok_dev, channels)
        return gather_prefix(
            update, start_t, me, groups, step_dev, steps_axis, partner_order
        )

    assert heads % per_dev == 0
    share = heads // per_dev
    first = me * per_dev
    head_ids = (first + jnp.arange(per_dev, dtype=jnp.int32)) % heads
    chosen = jnp.take(weight_heads, head_ids, axis=1)
    numer = jnp.einsum("cid,ild->cl", chosen, heads_out, preferred_element_type=jnp.float32)
    wide = heads_out.astype(jnp.float32)
    square = jnp.sum(wide * wide, axis=(0, 2))
    partial = jnp.concatenate([numer, square[None]], axis=0)
    partial = partial.reshape(channels + 1, groups, tok_dev)
    returned = lax.all_to_all(partial, "seq", split_axis=1, concat_axis=1, tiled=True)
    returned = returned.reshape(channels + 1, step_dev * branches, share, tok_dev)
    summed = jnp.sum(returned, axis=2).reshape(channels + 1, step_dev, branches, tok_dev)
    numer = jnp.transpose(summed[:channels], (1, 2, 0, 3))
    square_sum = summed[channels]
    root_mean = jnp.sqrt(square_sum / (H * HD) + 1e-06)
    drift = numer / root_mean[:, :, None, :]
    guided = drift[:, 1] + guide_scale * (drift[:, 0] - drift[:, 1])
    local_cum = jnp.cumsum(step_len[:, None, None] * guided, axis=0)
    return start_latent[None] + earlier_groups(local_cum, steps_axis) + local_cum


def solution(mesh):
    return jax.shard_map(
        on_device,
        mesh=mesh,
        in_specs=(
            P(("scene", "step"), None, None, "seq", None),
            P(("scene", "step"), None, None, "seq", None),
            P(("scene", "step"), None, None, "seq", None),
            P("scene", "seq"),
            P(),
            P(),
            P("scene"),
            P(),
            P(("scene", "step")),
        ),
        out_specs=P(("scene", "step"), None, "seq"),
        check_vma=False,
    )
```

```python
import jax
import jax.numpy as jnp
from jax import lax
from jax.sharding import PartitionSpec as P

HD = 128
H = 24


def lookup(table, index):
    count = table.shape[0]
    hits = index[..., None] == jnp.arange(count, dtype=jnp.int32)
    return jnp.sum(jnp.where(hits, table, jnp.zeros((), table.dtype)), axis=-1)


def attend(query_rows, key_rows, value_rows):
    scale = HD ** (-0.5)
    scores = (
        jnp.einsum("iqd,ikd->iqk", query_rows, key_rows, preferred_element_type=jnp.float32) * scale
    )
    expo = jnp.exp(scores - jnp.max(scores, axis=-1, keepdims=True))
    total = jnp.sum(expo, axis=-1, keepdims=True)
    weights = expo.astype(jnp.bfloat16)
    if isinstance(value_rows, list):
        out = None
        first = 0
        for block in value_rows:
            size = block.shape[1]
            part = jnp.einsum(
                "iqk,ikd->iqd",
                weights[:, :, first : first + size],
                block,
                preferred_element_type=jnp.float32,
            )
            out = part if out is None else out + part
            first += size
    else:
        out = jnp.einsum("iqk,ikd->iqd", weights, value_rows, preferred_element_type=jnp.float32)
    return (out / total).astype(jnp.bfloat16)


def xor_pairs(size, k):
    return [(i, i ^ k) for i in range(size)]


def gather_prefix(update, start, me, groups, step_dev, steps_axis, partner_order):
    local_steps = update.shape[0]
    if partner_order:
        ordered = update
    else:
        partners = me ^ jnp.arange(groups, dtype=jnp.int32)
        ordered = jnp.take(update, partners, axis=1)
    pieces = [ordered[:, 0]]
    sources = [me]
    for k in range(1, groups):
        pieces.append(lax.ppermute(ordered[:, k], "seq", xor_pairs(groups, k)))
        sources.append(me ^ k)
    zero = jnp.zeros((), jnp.float32)
    outs = []
    for s in range(step_dev):
        acc = None
        for piece, source in zip(pieces, sources):
            for t in range(local_steps):
                term = jnp.where(source * local_steps + t <= s, piece[t], zero)
                acc = term if acc is None else acc + term
        outs.append(acc)
    total = outs[-1]
    local_cum = lax.optimization_barrier(jnp.stack(outs) + start[None])
    position = lax.axis_index("step")
    earlier = jnp.zeros_like(total)
    if steps_axis & (steps_axis - 1) == 0:
        block = total
        k = 1
        while k < steps_axis:
            other = lax.ppermute(block, "step", xor_pairs(steps_axis, k))
            earlier = earlier + jnp.where(position & k != 0, other, zero)
            block = block + other
            k *= 2
    else:
        every_total = lax.all_gather(total[None], "step", axis=0, tiled=True)
        order = jnp.arange(steps_axis, dtype=jnp.int32)
        earlier = jnp.sum(jnp.where((order < position)[:, None, None], every_total, zero), axis=0)
    return jnp.transpose(local_cum + earlier[None], (0, 2, 1))


def earlier_groups(local_cum, steps_axis):
    every_total = lax.all_gather(local_cum[-1][None], "step", axis=0, tiled=True)
    position = lax.axis_index("step")
    order = jnp.arange(steps_axis, dtype=jnp.int32)
    earlier = jnp.sum(
        jnp.where((order < position)[:, None, None], every_total, jnp.zeros((), jnp.float32)),
        axis=0,
    )
    return earlier[None]


def on_device(
    queries, keys, values, start_latent, out_weight, cfg_table, cfg_index, step_table, time_index
):
    step_dev, branches, heads, tok_dev, head_size = queries.shape
    groups = lax.axis_size("seq")
    steps_axis = lax.axis_size("step")
    items = step_dev * branches * heads
    per_dev = items // groups
    length = tok_dev * groups
    channels = out_weight.shape[0]
    me = lax.axis_index("seq")

    chunks = [a.reshape(groups, per_dev, tok_dev, head_size) for a in (queries, keys, values)]
    whole_steps = per_dev % (branches * heads) == 0
    if whole_steps and groups & (groups - 1) == 0:
        arrived = {}
        for k in reversed(range(groups)):
            pieces = [lax.dynamic_index_in_dim(c, me ^ k, 0, keepdims=False) for c in chunks]
            if k:
                pieces = [lax.ppermute(p, "seq", xor_pairs(groups, k)) for p in pieces]
            arrived[k] = pieces
        gathered = [
            jnp.concatenate([arrived[k][i] for k in range(groups)], axis=1) for i in range(2)
        ]
        gathered.append([arrived[k][2] for k in range(groups)])
        partner_order = True
    else:
        stacked = jnp.stack(chunks, axis=1)
        gathered = lax.all_to_all(stacked, "seq", split_axis=0, concat_axis=3, tiled=True)
        gathered = gathered.reshape(3, per_dev, length, head_size)
        partner_order = False
    heads_out = attend(gathered[0], gathered[1], gathered[2])

    weight_heads = out_weight.reshape(channels, heads, head_size)
    guide_scale = lookup(cfg_table, cfg_index)[0]
    step_len = lookup(step_table, time_index)

    if whole_steps:
        local_steps = per_dev // (branches * heads)
        ho = heads_out.reshape(local_steps, branches, heads, length, head_size)
        wide = ho.astype(jnp.float32)
        square_sum = jnp.sum(wide * wide, axis=(2, 4))
        root_mean = jnp.sqrt(square_sum / (H * HD) + 1e-06)
        drift = (
            jnp.einsum("chd,sbhld->sblc", weight_heads, ho, preferred_element_type=jnp.float32)
            / root_mean[:, :, :, None]
        )
        owner = jnp.arange(step_dev, dtype=jnp.int32) // local_steps == me
        slot = jnp.arange(step_dev, dtype=jnp.int32) % local_steps
        mine = (owner[:, None] & (slot[:, None] == jnp.arange(local_steps)))[:, :, None, None]
        len_full = jnp.sum(
            jnp.where(mine, step_len[:, None, None, None], jnp.zeros((), jnp.float32)), axis=0
        )
        shape = (local_steps, length, channels)
        coef = lax.optimization_barrier(
            jnp.stack([jnp.broadcast_to(guide_scale, shape), jnp.broadcast_to(len_full, shape)])
        )
        scale_full, len_full = coef[0], coef[1]
        start_t = start_latent.T
        guided = drift[:, 1] + scale_full * (drift[:, 0] - drift[:, 1])
        update = len_full * guided
        update = update.reshape(local_steps, groups, tok_dev, channels)
        return gather_prefix(
            update, start_t, me, groups, step_dev, steps_axis, partner_order
        )

    assert heads % per_dev == 0
    share = heads // per_dev
    first = me * per_dev
    head_ids = (first + jnp.arange(per_dev, dtype=jnp.int32)) % heads
    chosen = jnp.take(weight_heads, head_ids, axis=1)
    numer = jnp.einsum("cid,ild->cl", chosen, heads_out, preferred_element_type=jnp.float32)
    wide = heads_out.astype(jnp.float32)
    square = jnp.sum(wide * wide, axis=(0, 2))
    partial = jnp.concatenate([numer, square[None]], axis=0)
    partial = partial.reshape(channels + 1, groups, tok_dev)
    returned = lax.all_to_all(partial, "seq", split_axis=1, concat_axis=1, tiled=True)
    returned = returned.reshape(channels + 1, step_dev * branches, share, tok_dev)
    summed = jnp.sum(returned, axis=2).reshape(channels + 1, step_dev, branches, tok_dev)
    numer = jnp.transpose(summed[:channels], (1, 2, 0, 3))
    square_sum = summed[channels]
    root_mean = jnp.sqrt(square_sum / (H * HD) + 1e-06)
    drift = numer / root_mean[:, :, None, :]
    guided = drift[:, 1] + guide_scale * (drift[:, 0] - drift[:, 1])
    local_cum = jnp.cumsum(step_len[:, None, None] * guided, axis=0)
    return start_latent[None] + earlier_groups(local_cum, steps_axis) + local_cum


def solution(mesh):
    return jax.shard_map(
        on_device,
        mesh=mesh,
        in_specs=(
            P(("scene", "step"), None, None, "seq", None),
            P(("scene", "step"), None, None, "seq", None),
            P(("scene", "step"), None, None, "seq", None),
            P("scene", "seq"),
            P(),
            P(),
            P("scene"),
            P(),
            P(("scene", "step")),
        ),
        out_specs=P(("scene", "step"), None, "seq"),
        check_vma=False,
    )
```

```python
import jax
import jax.numpy as jnp
from jax import lax
from jax.sharding import PartitionSpec as P

HD = 128
H = 24


def lookup(table, index):
    count = table.shape[0]
    hits = index[..., None] == jnp.arange(count, dtype=jnp.int32)
    return jnp.sum(jnp.where(hits, table, jnp.zeros((), table.dtype)), axis=-1)


def attend(query_rows, key_rows, value_rows):
    scale = HD ** (-0.5)
    scores = (
        jnp.einsum("iqd,ikd->iqk", query_rows, key_rows, preferred_element_type=jnp.float32) * scale
    )
    expo = jnp.exp(scores - jnp.max(scores, axis=-1, keepdims=True))
    total = jnp.sum(expo, axis=-1, keepdims=True)
    weights = expo.astype(jnp.bfloat16)
    if isinstance(value_rows, list):
        out = None
        first = 0
        for block in value_rows:
            size = block.shape[1]
            part = jnp.einsum(
                "iqk,ikd->iqd",
                weights[:, :, first : first + size],
                block,
                preferred_element_type=jnp.float32,
            )
            out = part if out is None else out + part
            first += size
    else:
        out = jnp.einsum("iqk,ikd->iqd", weights, value_rows, preferred_element_type=jnp.float32)
    return (out / total).astype(jnp.bfloat16)


def xor_pairs(size, k):
    return [(i, i ^ k) for i in range(size)]


def prefix_from_pieces(pieces, sources, start, step_dev, steps_axis):
    local_steps = pieces[0].shape[0]
    zero = jnp.zeros((), jnp.float32)
    outs = []
    for s in range(step_dev):
        acc = None
        for piece, source in zip(pieces, sources):
            for t in range(local_steps):
                term = jnp.where(source * local_steps + t <= s, piece[t], zero)
                acc = term if acc is None else acc + term
        outs.append(acc)
    total = outs[-1]
    local_cum = lax.optimization_barrier(jnp.stack(outs) + start[None])
    position = lax.axis_index("step")
    earlier = jnp.zeros_like(total)
    for k in range(1, steps_axis):
        other = lax.ppermute(total, "step", xor_pairs(steps_axis, k))
        earlier = earlier + jnp.where((position ^ k) < position, other, zero)
    return jnp.transpose(local_cum + earlier[None], (0, 2, 1))


def gather_prefix(update, start, me, groups, step_dev, steps_axis, partner_order):
    local_steps = update.shape[0]
    if partner_order:
        ordered = update
    else:
        partners = me ^ jnp.arange(groups, dtype=jnp.int32)
        ordered = jnp.take(update, partners, axis=1)
    pieces = [ordered[:, 0]]
    sources = [me]
    for k in range(1, groups):
        pieces.append(lax.ppermute(ordered[:, k], "seq", xor_pairs(groups, k)))
        sources.append(me ^ k)
    zero = jnp.zeros((), jnp.float32)
    outs = []
    for s in range(step_dev):
        acc = None
        for piece, source in zip(pieces, sources):
            for t in range(local_steps):
                term = jnp.where(source * local_steps + t <= s, piece[t], zero)
                acc = term if acc is None else acc + term
        outs.append(acc)
    total = outs[-1]
    local_cum = lax.optimization_barrier(jnp.stack(outs) + start[None])
    position = lax.axis_index("step")
    earlier = jnp.zeros_like(total)
    for k in range(1, steps_axis):
        other = lax.ppermute(total, "step", xor_pairs(steps_axis, k))
        earlier = earlier + jnp.where((position ^ k) < position, other, zero)
    return jnp.transpose(local_cum + earlier[None], (0, 2, 1))


def earlier_groups(local_cum, steps_axis):
    every_total = lax.all_gather(local_cum[-1][None], "step", axis=0, tiled=True)
    position = lax.axis_index("step")
    order = jnp.arange(steps_axis, dtype=jnp.int32)
    earlier = jnp.sum(
        jnp.where((order < position)[:, None, None], every_total, jnp.zeros((), jnp.float32)),
        axis=0,
    )
    return earlier[None]


def on_device(
    queries, keys, values, start_latent, out_weight, cfg_table, cfg_index, step_table, time_index
):
    step_dev, branches, heads, tok_dev, head_size = queries.shape
    groups = lax.axis_size("seq")
    steps_axis = lax.axis_size("step")
    items = step_dev * branches * heads
    per_dev = items // groups
    length = tok_dev * groups
    channels = out_weight.shape[0]
    me = lax.axis_index("seq")

    chunks = [a.reshape(groups, per_dev, tok_dev, head_size) for a in (queries, keys, values)]
    whole_steps = per_dev % (branches * heads) == 0
    if whole_steps and groups & (groups - 1) == 0:
        arrived = {}
        for k in reversed(range(groups)):
            pieces = [lax.dynamic_index_in_dim(c, me ^ k, 0, keepdims=False) for c in chunks]
            if k:
                pieces = [lax.ppermute(p, "seq", xor_pairs(groups, k)) for p in pieces]
            arrived[k] = pieces
        gathered = [
            jnp.concatenate([arrived[k][i] for k in range(groups)], axis=1) for i in range(2)
        ]
        gathered.append([arrived[k][2] for k in range(groups)])
        partner_order = True
    else:
        stacked = jnp.stack(chunks, axis=1)
        gathered = lax.all_to_all(stacked, "seq", split_axis=0, concat_axis=3, tiled=True)
        gathered = gathered.reshape(3, per_dev, length, head_size)
        partner_order = False
    if partner_order:
        far_q, cfg_table, cfg_index, step_table, time_index = lax.optimization_barrier(
            (arrived[groups - 1][0], cfg_table, cfg_index, step_table, time_index)
        )
        arrived[groups - 1][0] = far_q
        gathered[0] = jnp.concatenate([arrived[k][0] for k in range(groups)], axis=1)
    heads_out = attend(gathered[0], gathered[1], gathered[2])

    weight_heads = out_weight.reshape(channels, heads, head_size)
    guide_scale = lookup(cfg_table, cfg_index)[0]
    step_len = lookup(step_table, time_index)

    if whole_steps:
        local_steps = per_dev // (branches * heads)
        ho = heads_out.reshape(local_steps, branches, heads, length, head_size)
        wide = ho.astype(jnp.float32)
        square_sum = jnp.sum(wide * wide, axis=(2, 4))
        root_mean = jnp.sqrt(square_sum / (H * HD) + 1e-06)
        drift = (
            jnp.einsum("chd,sbhld->sblc", weight_heads, ho, preferred_element_type=jnp.float32)
            / root_mean[:, :, :, None]
        )
        start_t = start_latent.T
        if partner_order:
            pieces = drift.reshape(local_steps, branches, groups, tok_dev, channels)
            sent = [pieces[:, :, 0]]
            for k in range(1, groups):
                sent.append(lax.ppermute(pieces[:, :, k], "seq", xor_pairs(groups, k)))
            index = (me ^ jnp.arange(groups, dtype=jnp.int32))[:, None] * local_steps + jnp.arange(
                local_steps, dtype=jnp.int32
            )
            picks = index[:, :, None] == jnp.arange(step_dev, dtype=jnp.int32)
            lens = jnp.sum(jnp.where(picks, step_len, jnp.zeros((), jnp.float32)), axis=-1)
            shape = (groups, local_steps, tok_dev, channels)
            coef = lax.optimization_barrier(
                jnp.stack(
                    [jnp.broadcast_to(guide_scale, shape), jnp.broadcast_to(lens[:, :, None, None], shape)]
                )
            )
            updates = []
            for k in range(groups):
                guided = sent[k][:, 1] + coef[0, k] * (sent[k][:, 0] - sent[k][:, 1])
                updates.append(coef[1, k] * guided)
            sources = [me ^ k for k in range(groups)]
            return prefix_from_pieces(updates, sources, start_t, step_dev, steps_axis)
        owner = jnp.arange(step_dev, dtype=jnp.int32) // local_steps == me
        slot = jnp.arange(step_dev, dtype=jnp.int32) % local_steps
        mine = (owner[:, None] & (slot[:, None] == jnp.arange(local_steps)))[:, :, None, None]
        len_full = jnp.sum(
            jnp.where(mine, step_len[:, None, None, None], jnp.zeros((), jnp.float32)), axis=0
        )
        shape = (local_steps, length, channels)
        coef = lax.optimization_barrier(
            jnp.stack([jnp.broadcast_to(guide_scale, shape), jnp.broadcast_to(len_full, shape)])
        )
        scale_full, len_full = coef[0], coef[1]
        guided = drift[:, 1] + scale_full * (drift[:, 0] - drift[:, 1])
        update = len_full * guided
        update = update.reshape(local_steps, groups, tok_dev, channels)
        return gather_prefix(
            update, start_t, me, groups, step_dev, steps_axis, partner_order
        )

    assert heads % per_dev == 0
    share = heads // per_dev
    first = me * per_dev
    head_ids = (first + jnp.arange(per_dev, dtype=jnp.int32)) % heads
    chosen = jnp.take(weight_heads, head_ids, axis=1)
    numer = jnp.einsum("cid,ild->cl", chosen, heads_out, preferred_element_type=jnp.float32)
    wide = heads_out.astype(jnp.float32)
    square = jnp.sum(wide * wide, axis=(0, 2))
    partial = jnp.concatenate([numer, square[None]], axis=0)
    partial = partial.reshape(channels + 1, groups, tok_dev)
    returned = lax.all_to_all(partial, "seq", split_axis=1, concat_axis=1, tiled=True)
    returned = returned.reshape(channels + 1, step_dev * branches, share, tok_dev)
    summed = jnp.sum(returned, axis=2).reshape(channels + 1, step_dev, branches, tok_dev)
    numer = jnp.transpose(summed[:channels], (1, 2, 0, 3))
    square_sum = summed[channels]
    root_mean = jnp.sqrt(square_sum / (H * HD) + 1e-06)
    drift = numer / root_mean[:, :, None, :]
    guided = drift[:, 1] + guide_scale * (drift[:, 0] - drift[:, 1])
    local_cum = jnp.cumsum(step_len[:, None, None] * guided, axis=0)
    return start_latent[None] + earlier_groups(local_cum, steps_axis) + local_cum


def solution(mesh):
    return jax.shard_map(
        on_device,
        mesh=mesh,
        in_specs=(
            P(("scene", "step"), None, None, "seq", None),
            P(("scene", "step"), None, None, "seq", None),
            P(("scene", "step"), None, None, "seq", None),
            P("scene", "seq"),
            P(),
            P(),
            P("scene"),
            P(),
            P(("scene", "step")),
        ),
        out_specs=P(("scene", "step"), None, "seq"),
        check_vma=False,
    )
```

```python
import jax
import jax.numpy as jnp
from jax import lax
from jax.sharding import PartitionSpec as P

HD = 128
H = 24


def lookup(table, index):
    count = table.shape[0]
    hits = index[..., None] == jnp.arange(count, dtype=jnp.int32)
    return jnp.sum(jnp.where(hits, table, jnp.zeros((), table.dtype)), axis=-1)


def attend(query_rows, key_rows, value_rows):
    scale = HD ** (-0.5)
    scores = (
        jnp.einsum("iqd,ikd->iqk", query_rows, key_rows, preferred_element_type=jnp.float32) * scale
    )
    expo = jnp.exp(scores - jnp.max(scores, axis=-1, keepdims=True))
    total = jnp.sum(expo, axis=-1, keepdims=True)
    weights = expo.astype(jnp.bfloat16)
    if isinstance(value_rows, list):
        out = None
        first = 0
        for block in value_rows:
            size = block.shape[1]
            part = jnp.einsum(
                "iqk,ikd->iqd",
                weights[:, :, first : first + size],
                block,
                preferred_element_type=jnp.float32,
            )
            out = part if out is None else out + part
            first += size
    else:
        out = jnp.einsum("iqk,ikd->iqd", weights, value_rows, preferred_element_type=jnp.float32)
    return (out / total).astype(jnp.bfloat16)


def xor_pairs(size, k):
    return [(i, i ^ k) for i in range(size)]


def prefix_from_pieces(pieces, sources, start, step_dev, steps_axis):
    local_steps = pieces[0].shape[0]
    zero = jnp.zeros((), jnp.float32)
    outs = []
    for s in range(step_dev):
        acc = None
        for piece, source in zip(pieces, sources):
            for t in range(local_steps):
                term = jnp.where(source * local_steps + t <= s, piece[t], zero)
                acc = term if acc is None else acc + term
        outs.append(acc)
    total = outs[-1]
    local_cum = lax.optimization_barrier(jnp.stack(outs) + start[None])
    position = lax.axis_index("step")
    earlier = jnp.zeros_like(total)
    for k in range(1, steps_axis):
        other = lax.ppermute(total, "step", xor_pairs(steps_axis, k))
        earlier = earlier + jnp.where((position ^ k) < position, other, zero)
    return jnp.transpose(local_cum + earlier[None], (0, 2, 1))


def gather_prefix(update, start, me, groups, step_dev, steps_axis, partner_order):
    local_steps = update.shape[0]
    if partner_order:
        ordered = update
    else:
        partners = me ^ jnp.arange(groups, dtype=jnp.int32)
        ordered = jnp.take(update, partners, axis=1)
    pieces = [ordered[:, 0]]
    sources = [me]
    for k in range(1, groups):
        pieces.append(lax.ppermute(ordered[:, k], "seq", xor_pairs(groups, k)))
        sources.append(me ^ k)
    zero = jnp.zeros((), jnp.float32)
    outs = []
    for s in range(step_dev):
        acc = None
        for piece, source in zip(pieces, sources):
            for t in range(local_steps):
                term = jnp.where(source * local_steps + t <= s, piece[t], zero)
                acc = term if acc is None else acc + term
        outs.append(acc)
    total = outs[-1]
    local_cum = lax.optimization_barrier(jnp.stack(outs) + start[None])
    position = lax.axis_index("step")
    earlier = jnp.zeros_like(total)
    for k in range(1, steps_axis):
        other = lax.ppermute(total, "step", xor_pairs(steps_axis, k))
        earlier = earlier + jnp.where((position ^ k) < position, other, zero)
    return jnp.transpose(local_cum + earlier[None], (0, 2, 1))


def earlier_groups(local_cum, steps_axis):
    every_total = lax.all_gather(local_cum[-1][None], "step", axis=0, tiled=True)
    position = lax.axis_index("step")
    order = jnp.arange(steps_axis, dtype=jnp.int32)
    earlier = jnp.sum(
        jnp.where((order < position)[:, None, None], every_total, jnp.zeros((), jnp.float32)),
        axis=0,
    )
    return earlier[None]


def on_device(
    queries, keys, values, start_latent, out_weight, cfg_table, cfg_index, step_table, time_index
):
    step_dev, branches, heads, tok_dev, head_size = queries.shape
    groups = lax.axis_size("seq")
    steps_axis = lax.axis_size("step")
    items = step_dev * branches * heads
    per_dev = items // groups
    length = tok_dev * groups
    channels = out_weight.shape[0]
    me = lax.axis_index("seq")

    chunks = [a.reshape(groups, per_dev, tok_dev, head_size) for a in (queries, keys, values)]
    whole_steps = per_dev % (branches * heads) == 0
    if whole_steps and groups & (groups - 1) == 0:
        arrived = {}
        for k in reversed(range(groups)):
            pieces = [lax.dynamic_index_in_dim(c, me ^ k, 0, keepdims=False) for c in chunks]
            if k:
                pieces = [lax.ppermute(p, "seq", xor_pairs(groups, k)) for p in pieces]
            arrived[k] = pieces
        gathered = [
            jnp.concatenate([arrived[k][i] for k in range(groups)], axis=1) for i in range(2)
        ]
        gathered.append([arrived[k][2] for k in range(groups)])
        partner_order = True
    else:
        stacked = jnp.stack(chunks, axis=1)
        gathered = lax.all_to_all(stacked, "seq", split_axis=0, concat_axis=3, tiled=True)
        gathered = gathered.reshape(3, per_dev, length, head_size)
        partner_order = False
    if partner_order:
        far_q, step_table, time_index = lax.optimization_barrier(
            (arrived[groups - 1][0], step_table, time_index)
        )
        arrived[groups - 1][0] = far_q
        gathered[0] = jnp.concatenate([arrived[k][0] for k in range(groups)], axis=1)
    heads_out = attend(gathered[0], gathered[1], gathered[2])

    weight_heads = out_weight.reshape(channels, heads, head_size)
    guide_scale = lookup(cfg_table, cfg_index)[0]
    step_len = lookup(step_table, time_index)

    if whole_steps:
        local_steps = per_dev // (branches * heads)
        ho = heads_out.reshape(local_steps, branches, heads, length, head_size)
        wide = ho.astype(jnp.float32)
        square_sum = jnp.sum(wide * wide, axis=(2, 4))
        root_mean = jnp.sqrt(square_sum / (H * HD) + 1e-06)
        drift = (
            jnp.einsum("chd,sbhld->sblc", weight_heads, ho, preferred_element_type=jnp.float32)
            / root_mean[:, :, :, None]
        )
        start_t = start_latent.T
        if partner_order:
            pieces = drift.reshape(local_steps, branches, groups, tok_dev, channels)
            sent = [pieces[:, :, 0]]
            for k in range(1, groups):
                sent.append(lax.ppermute(pieces[:, :, k], "seq", xor_pairs(groups, k)))
            index = (me ^ jnp.arange(groups, dtype=jnp.int32))[:, None] * local_steps + jnp.arange(
                local_steps, dtype=jnp.int32
            )
            picks = index[:, :, None] == jnp.arange(step_dev, dtype=jnp.int32)
            lens = jnp.sum(jnp.where(picks, step_len, jnp.zeros((), jnp.float32)), axis=-1)
            shape = (groups, local_steps, tok_dev, channels)
            coef = lax.optimization_barrier(
                jnp.stack(
                    [jnp.broadcast_to(guide_scale, shape), jnp.broadcast_to(lens[:, :, None, None], shape)]
                )
            )
            updates = []
            for k in range(groups):
                guided = sent[k][:, 1] + coef[0, k] * (sent[k][:, 0] - sent[k][:, 1])
                updates.append(coef[1, k] * guided)
            sources = [me ^ k for k in range(groups)]
            return prefix_from_pieces(updates, sources, start_t, step_dev, steps_axis)
        owner = jnp.arange(step_dev, dtype=jnp.int32) // local_steps == me
        slot = jnp.arange(step_dev, dtype=jnp.int32) % local_steps
        mine = (owner[:, None] & (slot[:, None] == jnp.arange(local_steps)))[:, :, None, None]
        len_full = jnp.sum(
            jnp.where(mine, step_len[:, None, None, None], jnp.zeros((), jnp.float32)), axis=0
        )
        shape = (local_steps, length, channels)
        coef = lax.optimization_barrier(
            jnp.stack([jnp.broadcast_to(guide_scale, shape), jnp.broadcast_to(len_full, shape)])
        )
        scale_full, len_full = coef[0], coef[1]
        guided = drift[:, 1] + scale_full * (drift[:, 0] - drift[:, 1])
        update = len_full * guided
        update = update.reshape(local_steps, groups, tok_dev, channels)
        return gather_prefix(
            update, start_t, me, groups, step_dev, steps_axis, partner_order
        )

    assert heads % per_dev == 0
    share = heads // per_dev
    first = me * per_dev
    head_ids = (first + jnp.arange(per_dev, dtype=jnp.int32)) % heads
    chosen = jnp.take(weight_heads, head_ids, axis=1)
    numer = jnp.einsum("cid,ild->cl", chosen, heads_out, preferred_element_type=jnp.float32)
    wide = heads_out.astype(jnp.float32)
    square = jnp.sum(wide * wide, axis=(0, 2))
    partial = jnp.concatenate([numer, square[None]], axis=0)
    partial = partial.reshape(channels + 1, groups, tok_dev)
    returned = lax.all_to_all(partial, "seq", split_axis=1, concat_axis=1, tiled=True)
    returned = returned.reshape(channels + 1, step_dev * branches, share, tok_dev)
    summed = jnp.sum(returned, axis=2).reshape(channels + 1, step_dev, branches, tok_dev)
    numer = jnp.transpose(summed[:channels], (1, 2, 0, 3))
    square_sum = summed[channels]
    root_mean = jnp.sqrt(square_sum / (H * HD) + 1e-06)
    drift = numer / root_mean[:, :, None, :]
    guided = drift[:, 1] + guide_scale * (drift[:, 0] - drift[:, 1])
    local_cum = jnp.cumsum(step_len[:, None, None] * guided, axis=0)
    return start_latent[None] + earlier_groups(local_cum, steps_axis) + local_cum


def solution(mesh):
    return jax.shard_map(
        on_device,
        mesh=mesh,
        in_specs=(
            P(("scene", "step"), None, None, "seq", None),
            P(("scene", "step"), None, None, "seq", None),
            P(("scene", "step"), None, None, "seq", None),
            P("scene", "seq"),
            P(),
            P(),
            P("scene"),
            P(),
            P(("scene", "step")),
        ),
        out_specs=P(("scene", "step"), None, "seq"),
        check_vma=False,
    )
```

```python
import jax
import jax.numpy as jnp
from jax import lax
from jax.sharding import PartitionSpec as P

HD = 128
H = 24


def lookup(table, index):
    count = table.shape[0]
    hits = index[..., None] == jnp.arange(count, dtype=jnp.int32)
    return jnp.sum(jnp.where(hits, table, jnp.zeros((), table.dtype)), axis=-1)


def attend(query_rows, key_rows, value_rows):
    scale = HD ** (-0.5)
    scores = (
        jnp.einsum("iqd,ikd->iqk", query_rows, key_rows, preferred_element_type=jnp.float32) * scale
    )
    expo = jnp.exp(scores - jnp.max(scores, axis=-1, keepdims=True))
    total = jnp.sum(expo, axis=-1, keepdims=True)
    weights = expo.astype(jnp.bfloat16)
    if isinstance(value_rows, list):
        out = None
        first = 0
        for block in value_rows:
            size = block.shape[1]
            part = jnp.einsum(
                "iqk,ikd->iqd",
                weights[:, :, first : first + size],
                block,
                preferred_element_type=jnp.float32,
            )
            out = part if out is None else out + part
            first += size
    else:
        out = jnp.einsum("iqk,ikd->iqd", weights, value_rows, preferred_element_type=jnp.float32)
    return (out / total).astype(jnp.bfloat16)


def xor_pairs(size, k):
    return [(i, i ^ k) for i in range(size)]


def prefix_from_pieces(pieces, sources, start, step_dev, steps_axis):
    local_steps = pieces[0].shape[0]
    zero = jnp.zeros((), jnp.float32)
    outs = []
    for s in range(step_dev):
        acc = None
        for piece, source in zip(pieces, sources):
            for t in range(local_steps):
                term = jnp.where(source * local_steps + t <= s, piece[t], zero)
                acc = term if acc is None else acc + term
        outs.append(acc)
    total = outs[-1]
    local_cum = lax.optimization_barrier(jnp.stack(outs) + start[None])
    position = lax.axis_index("step")
    earlier = jnp.zeros_like(total)
    for k in range(1, steps_axis):
        other = lax.ppermute(total, "step", xor_pairs(steps_axis, k))
        earlier = earlier + jnp.where((position ^ k) < position, other, zero)
    return jnp.transpose(local_cum + earlier[None], (0, 2, 1))


def gather_prefix(update, start, me, groups, step_dev, steps_axis, partner_order):
    local_steps = update.shape[0]
    if partner_order:
        ordered = update
    else:
        partners = me ^ jnp.arange(groups, dtype=jnp.int32)
        ordered = jnp.take(update, partners, axis=1)
    pieces = [ordered[:, 0]]
    sources = [me]
    for k in range(1, groups):
        pieces.append(lax.ppermute(ordered[:, k], "seq", xor_pairs(groups, k)))
        sources.append(me ^ k)
    zero = jnp.zeros((), jnp.float32)
    outs = []
    for s in range(step_dev):
        acc = None
        for piece, source in zip(pieces, sources):
            for t in range(local_steps):
                term = jnp.where(source * local_steps + t <= s, piece[t], zero)
                acc = term if acc is None else acc + term
        outs.append(acc)
    total = outs[-1]
    local_cum = lax.optimization_barrier(jnp.stack(outs) + start[None])
    position = lax.axis_index("step")
    earlier = jnp.zeros_like(total)
    for k in range(1, steps_axis):
        other = lax.ppermute(total, "step", xor_pairs(steps_axis, k))
        earlier = earlier + jnp.where((position ^ k) < position, other, zero)
    return jnp.transpose(local_cum + earlier[None], (0, 2, 1))


def earlier_groups(local_cum, steps_axis):
    every_total = lax.all_gather(local_cum[-1][None], "step", axis=0, tiled=True)
    position = lax.axis_index("step")
    order = jnp.arange(steps_axis, dtype=jnp.int32)
    earlier = jnp.sum(
        jnp.where((order < position)[:, None, None], every_total, jnp.zeros((), jnp.float32)),
        axis=0,
    )
    return earlier[None]


def on_device(
    queries, keys, values, start_latent, out_weight, cfg_table, cfg_index, step_table, time_index
):
    step_dev, branches, heads, tok_dev, head_size = queries.shape
    groups = lax.axis_size("seq")
    steps_axis = lax.axis_size("step")
    items = step_dev * branches * heads
    per_dev = items // groups
    length = tok_dev * groups
    channels = out_weight.shape[0]
    me = lax.axis_index("seq")

    chunks = [a.reshape(groups, per_dev, tok_dev, head_size) for a in (queries, keys, values)]
    whole_steps = per_dev % (branches * heads) == 0
    if whole_steps and groups & (groups - 1) == 0:
        sliced = {
            k: [lax.dynamic_index_in_dim(c, me ^ k, 0, keepdims=False) for c in chunks]
            for k in range(groups)
        }
        if groups > 2:
            near, far = lax.optimization_barrier((sliced[1], sliced[groups - 1]))
            sliced[1] = near
        arrived = {}
        for k in reversed(range(groups)):
            pieces = sliced[k]
            if k:
                pieces = [lax.ppermute(p, "seq", xor_pairs(groups, k)) for p in pieces]
            arrived[k] = pieces
        gathered = [
            jnp.concatenate([arrived[k][i] for k in range(groups)], axis=1) for i in range(2)
        ]
        gathered.append([arrived[k][2] for k in range(groups)])
        partner_order = True
    else:
        stacked = jnp.stack(chunks, axis=1)
        gathered = lax.all_to_all(stacked, "seq", split_axis=0, concat_axis=3, tiled=True)
        gathered = gathered.reshape(3, per_dev, length, head_size)
        partner_order = False
    if partner_order:
        far_q, cfg_table, cfg_index, step_table, time_index = lax.optimization_barrier(
            (arrived[groups - 1][0], cfg_table, cfg_index, step_table, time_index)
        )
        arrived[groups - 1][0] = far_q
        gathered[0] = jnp.concatenate([arrived[k][0] for k in range(groups)], axis=1)
    heads_out = attend(gathered[0], gathered[1], gathered[2])

    weight_heads = out_weight.reshape(channels, heads, head_size)
    guide_scale = lookup(cfg_table, cfg_index)[0]
    step_len = lookup(step_table, time_index)

    if whole_steps:
        local_steps = per_dev // (branches * heads)
        ho = heads_out.reshape(local_steps, branches, heads, length, head_size)
        wide = ho.astype(jnp.float32)
        square_sum = jnp.sum(wide * wide, axis=(2, 4))
        root_mean = jnp.sqrt(square_sum / (H * HD) + 1e-06)
        drift = (
            jnp.einsum("chd,sbhld->sblc", weight_heads, ho, preferred_element_type=jnp.float32)
            / root_mean[:, :, :, None]
        )
        start_t = start_latent.T
        if partner_order:
            pieces = drift.reshape(local_steps, branches, groups, tok_dev, channels)
            sent = [pieces[:, :, 0]]
            for k in range(1, groups):
                sent.append(lax.ppermute(pieces[:, :, k], "seq", xor_pairs(groups, k)))
            index = (me ^ jnp.arange(groups, dtype=jnp.int32))[:, None] * local_steps + jnp.arange(
                local_steps, dtype=jnp.int32
            )
            picks = index[:, :, None] == jnp.arange(step_dev, dtype=jnp.int32)
            lens = jnp.sum(jnp.where(picks, step_len, jnp.zeros((), jnp.float32)), axis=-1)
            shape = (groups, local_steps, tok_dev, channels)
            coef = lax.optimization_barrier(
                jnp.stack(
                    [jnp.broadcast_to(guide_scale, shape), jnp.broadcast_to(lens[:, :, None, None], shape)]
                )
            )
            updates = []
            for k in range(groups):
                guided = sent[k][:, 1] + coef[0, k] * (sent[k][:, 0] - sent[k][:, 1])
                updates.append(coef[1, k] * guided)
            sources = [me ^ k for k in range(groups)]
            return prefix_from_pieces(updates, sources, start_t, step_dev, steps_axis)
        owner = jnp.arange(step_dev, dtype=jnp.int32) // local_steps == me
        slot = jnp.arange(step_dev, dtype=jnp.int32) % local_steps
        mine = (owner[:, None] & (slot[:, None] == jnp.arange(local_steps)))[:, :, None, None]
        len_full = jnp.sum(
            jnp.where(mine, step_len[:, None, None, None], jnp.zeros((), jnp.float32)), axis=0
        )
        shape = (local_steps, length, channels)
        coef = lax.optimization_barrier(
            jnp.stack([jnp.broadcast_to(guide_scale, shape), jnp.broadcast_to(len_full, shape)])
        )
        scale_full, len_full = coef[0], coef[1]
        guided = drift[:, 1] + scale_full * (drift[:, 0] - drift[:, 1])
        update = len_full * guided
        update = update.reshape(local_steps, groups, tok_dev, channels)
        return gather_prefix(
            update, start_t, me, groups, step_dev, steps_axis, partner_order
        )

    assert heads % per_dev == 0
    share = heads // per_dev
    first = me * per_dev
    head_ids = (first + jnp.arange(per_dev, dtype=jnp.int32)) % heads
    chosen = jnp.take(weight_heads, head_ids, axis=1)
    numer = jnp.einsum("cid,ild->cl", chosen, heads_out, preferred_element_type=jnp.float32)
    wide = heads_out.astype(jnp.float32)
    square = jnp.sum(wide * wide, axis=(0, 2))
    partial = jnp.concatenate([numer, square[None]], axis=0)
    partial = partial.reshape(channels + 1, groups, tok_dev)
    returned = lax.all_to_all(partial, "seq", split_axis=1, concat_axis=1, tiled=True)
    returned = returned.reshape(channels + 1, step_dev * branches, share, tok_dev)
    summed = jnp.sum(returned, axis=2).reshape(channels + 1, step_dev, branches, tok_dev)
    numer = jnp.transpose(summed[:channels], (1, 2, 0, 3))
    square_sum = summed[channels]
    root_mean = jnp.sqrt(square_sum / (H * HD) + 1e-06)
    drift = numer / root_mean[:, :, None, :]
    guided = drift[:, 1] + guide_scale * (drift[:, 0] - drift[:, 1])
    local_cum = jnp.cumsum(step_len[:, None, None] * guided, axis=0)
    return start_latent[None] + earlier_groups(local_cum, steps_axis) + local_cum


def solution(mesh):
    return jax.shard_map(
        on_device,
        mesh=mesh,
        in_specs=(
            P(("scene", "step"), None, None, "seq", None),
            P(("scene", "step"), None, None, "seq", None),
            P(("scene", "step"), None, None, "seq", None),
            P("scene", "seq"),
            P(),
            P(),
            P("scene"),
            P(),
            P(("scene", "step")),
        ),
        out_specs=P(("scene", "step"), None, "seq"),
        check_vma=False,
    )
```
